1024 devices in a mesh: seq: 16 (over z_lo), head: 4 (over z_hi, core), fsdp: 16 (over x, y).
Axes of the slice: x: 4, y: 4, z: 32 (z_hi: 2, z_lo: 16; z = z_hi * 16 + z_lo), core: 2. Of those that a mesh axis runs over, the one named last changes fastest.
Arguments:
- queries: bfloat16 [16, 6144, 1536], P('fsdp', 'seq', 'head'), may hold values from -40 to 40
- keys: bfloat16 [16, 6144, 1536], P('fsdp', 'seq', 'head'), may hold values from -40 to 40
- values: bfloat16 [16, 6144, 1536], P('fsdp', 'seq', 'head'), may hold values from -6 to 6
- q_gain: float32 [128], replicated, may hold values from 1.2 to 5.5
- k_gain: float32 [128], replicated, may hold values from 1.2 to 5.5
- d_out: bfloat16 [16, 6144, 1536], P('fsdp', 'seq', 'head'), may hold values from -18 to 18
- window: int32 [16, 16, 3], P('fsdp', 'seq'), may hold values from -1 to 15, as said below
Outputs:
- attended: bfloat16 [16, 6144, 1536], P('fsdp', 'seq', 'head')
- grad_queries: bfloat16 [16, 6144, 1536], P('fsdp', 'seq', 'head')
- grad_keys: bfloat16 [16, 6144, 1536], P('fsdp', 'seq', 'head')
- grad_values: bfloat16 [16, 6144, 1536], P('fsdp', 'seq', 'head')
- q_gain_grad: float32 [128], replicated
- k_gain_grad: float32 [128], replicated
The draws below stay inside these ranges and needn't reach their ends.
Inputs may be any that keep to these rules, and one draw needn't show every extreme that they name: `window`: row (s, t) names tile t, and may name t - 1 and t + 1 where those tiles exist, each at most once and in any order; its other entries are -1. In every sample some row names three tiles.
All inputs are finite; a program needn't handle non-finite values.
Results may differ from the reference program's by a relative error of at most 0.013.
The reference program's roundings to bfloat16 on the way count: a program that leaves them out, or rounds other values in their place, can miss the bound.
Values may be sent and summed in bfloat16 or wider, within the bound.
No kernel may reach another device: no remote copies, remote signals or barrier semaphores. Data moves between devices by JAX's collectives and lax.ppermute only.
A program may use at most 32 MiB of HBM per device.

```python
import math
import jax
import jax.numpy as jnp
from jax import lax

DH = 128
HEADS = 12
TILE = 384
SAMPLES = 16
TILES = 16
TOKENS = 6144
HD = 1536


def rough_field(key, salt):
    base_key, row_key, col_key = jax.random.split(jax.random.fold_in(key, salt), 3)
    base_field = jax.random.normal(base_key, (SAMPLES, TOKENS, HD), jnp.float32)
    row_scale = jnp.exp(jax.random.uniform(row_key, (SAMPLES, TOKENS, 1), jnp.float32, math.log(0.3), math.log(3.0)))
    col_scale = jnp.exp(jax.random.uniform(col_key, (1, 1, HD), jnp.float32, math.log(0.3), math.log(3.0)))
    return base_field * row_scale * col_scale


def draw_queries(key, part):
    field = rough_field(key, 11)
    return jnp.clip(field, -40.0, 40.0).astype(jnp.bfloat16)


def draw_keys(key, part):
    field = rough_field(key, 12)
    return jnp.clip(field, -40.0, 40.0).astype(jnp.bfloat16)


def gain_law(key):
    return jnp.exp(jax.random.uniform(key, (DH,), jnp.float32, math.log(1.2), math.log(2.4)))


def draw_q_gain(key, part):
    return gain_law(jax.random.fold_in(key, 21))


def draw_k_gain(key, part):
    return gain_law(jax.random.fold_in(key, 22))


def draw_d_out(key, part):
    noise_key = jax.random.fold_in(key, 31)
    base_field = jax.random.normal(noise_key, (SAMPLES, TOKENS, HD), jnp.float32)
    tile_pos = (jnp.arange(TOKENS) // TILE).astype(jnp.float32) / max(TILES - 1, 1)
    head_pos = (jnp.arange(HD) // DH).astype(jnp.float32) / max(HEADS - 1, 1)
    sample_pos = jnp.arange(SAMPLES).astype(jnp.float32) / max(SAMPLES - 1, 1)
    rise_factor = (1.0 + 2.0 * sample_pos)[:, None, None] * (1.0 + 2.0 * tile_pos)[None, :, None] * (1.0 + 2.0 * head_pos)[None, None, :] / 9.0
    return jnp.clip(base_field * rise_factor, -18.0, 18.0).astype(jnp.bfloat16)


def draw_window(key, part):
    first_key, second_key, third_key, fourth_key = jax.random.split(jax.random.fold_in(key, 41), 4)
    position = jnp.arange(TILES, dtype=jnp.int32)[None, :]
    left_flag = jax.random.randint(first_key, (SAMPLES, TILES), 0, 2)
    right_flag = jax.random.randint(second_key, (SAMPLES, TILES), 0, 2)
    forced = jax.random.randint(third_key, (SAMPLES, 1), 1, TILES - 1)
    chosen = (position == forced).astype(jnp.int32)
    left_flag = jnp.maximum(left_flag, chosen)
    right_flag = jnp.maximum(right_flag, chosen)
    lower = jnp.where((left_flag > 0) & (position > 0), position - 1, -1)
    upper = jnp.where((right_flag > 0) & (position < TILES - 1), position + 1, -1)
    middle = jnp.broadcast_to(position, (SAMPLES, TILES))
    stacked = jnp.stack([lower, middle, upper], axis=-1)
    turn = jax.random.randint(fourth_key, (SAMPLES, TILES, 1), 0, 3)
    order = (jnp.arange(3, dtype=jnp.int32)[None, None, :] + turn) % 3
    return jnp.take_along_axis(stacked, order, axis=-1).astype(jnp.int32)


def levels(rng, extent, shards, least, high):
    def one(dim, shards_of):
        heights = jax.random.uniform(jax.random.fold_in(jax.random.fold_in(rng, 6), dim), (shards_of,), jnp.float32, least / len(shards), high / len(shards))
        return jnp.repeat(jnp.exp(heights), extent[dim] // shards_of).reshape((-1,) + (1,) * (len(extent) - dim - 1))

    factor_of = one(*shards[0])
    for cut in shards[1:]:
        factor_of = factor_of * one(*cut)
    return factor_of


def bell_draw(rng, shape, scale, limit, cuts=(), kind=jnp.bfloat16):
    drawn = scale * jax.random.normal(rng, shape, jnp.float32)
    if cuts:
        drawn = drawn * levels(rng, shape, cuts, -0.22, 0.18)
    return jnp.clip(drawn, -limit, limit).astype(kind)


def setup_inputs(seed: int = 0) -> dict:
    key_of = jax.random.split(jax.random.key(seed), 8)
    return {
        "queries": draw_queries(jax.random.fold_in(key_of[7], 71), 0),
        "keys": draw_keys(jax.random.fold_in(key_of[7], 71), 0),
        "values": bell_draw(key_of[2], (SAMPLES, TOKENS, HD), 1.0, 6.0, ((0, 16), (1, 16), (2, 4))),
        "q_gain": draw_q_gain(jax.random.fold_in(key_of[7], 71), 0),
        "k_gain": draw_k_gain(jax.random.fold_in(key_of[7], 71), 0),
        "d_out": draw_d_out(jax.random.fold_in(key_of[7], 71), 0),
        "window": draw_window(jax.random.fold_in(key_of[7], 71), 0),
    }


EPSILON = 1e-06

def normalize(raw_rows, gain_vector):
    shaped = raw_rows.astype(jnp.float32).reshape(raw_rows.shape[0], raw_rows.shape[1], -1, gain_vector.shape[0])
    factor = lax.rsqrt(lax.optimization_barrier(jnp.mean(shaped * shaped, axis=-1, keepdims=True)) + EPSILON)
    unit_rows = shaped * factor
    return (unit_rows, factor, (unit_rows * gain_vector).astype(jnp.bfloat16))

def restore(grad_norm, unit_rows, factor, gain_vector):
    scaled = grad_norm * gain_vector
    inner_mean = lax.optimization_barrier(jnp.mean(scaled * unit_rows, axis=-1, keepdims=True))
    return factor * (scaled - unit_rows * inner_mean)

def rounded(term):
    return lax.optimization_barrier(term.astype(jnp.bfloat16)).astype(jnp.float32)

def beside_all(blocks):
    zero_tile = jnp.zeros_like(blocks[:1])
    padded = jnp.concatenate([zero_tile, blocks, zero_tile], axis=0)
    return jnp.concatenate([padded[:-2], padded[1:-1], padded[2:]], axis=1)

def gather_back(terms, tile_count):
    blocks = terms.reshape(tile_count, 3, TILE, terms.shape[2], terms.shape[3])
    zero_tile = jnp.zeros_like(blocks[:1, 0])
    from_right = jnp.concatenate([blocks[1:, 0], zero_tile], axis=0)
    from_left = jnp.concatenate([zero_tile, blocks[:-1, 2]], axis=0)
    return blocks[:, 1] + rounded(from_left) + rounded(from_right)

def one_sample(operands, q_gain, k_gain):
    queries, keys, values, d_out, window = operands
    tile_count = queries.shape[0] // TILE
    columns = queries.shape[1]
    score_scale = 1.0 / math.sqrt(DH)
    q_unit, q_factor, q_norm = normalize(queries.reshape(tile_count, TILE, columns), q_gain)
    k_unit, k_factor, k_norm = normalize(keys.reshape(tile_count, TILE, columns), k_gain)
    value_rows = values.reshape(tile_count, TILE, HEADS, DH)
    grad_out = d_out.reshape(tile_count, TILE, HEADS, DH)
    key_all = beside_all(k_norm)
    value_all = beside_all(value_rows)
    targets = jnp.arange(tile_count, dtype=jnp.int32)[:, None] + jnp.arange(3, dtype=jnp.int32)[None, :] - 1
    block_flags = jnp.any(window[:, None, :] == targets[:, :, None], axis=-1) & (targets >= 0) & (targets < tile_count)
    allowed = jnp.repeat(block_flags, TILE, axis=1)
    scores = jnp.einsum('tqhd,tkhd->thqk', q_norm.astype(jnp.float32), key_all.astype(jnp.float32)) * score_scale
    scores = jnp.where(allowed[:, None, None, :], scores, -jnp.inf)
    row_max = lax.optimization_barrier(jnp.max(scores, axis=-1, keepdims=True))
    row_sum = lax.optimization_barrier(jnp.sum(jnp.exp(scores - row_max), axis=-1, keepdims=True))
    log_total = row_max + jnp.log(row_sum)
    attn_weights = jnp.exp(scores - log_total).astype(jnp.bfloat16)
    attended = jnp.einsum('thqk,tkhd->tqhd', attn_weights.astype(jnp.float32), value_all.astype(jnp.float32)).astype(jnp.bfloat16)
    row_inner = lax.optimization_barrier(jnp.sum(grad_out.astype(jnp.float32) * attended.astype(jnp.float32), axis=-1))
    row_inner = jnp.moveaxis(row_inner, 2, 1)[..., None]
    grad_weights = jnp.einsum('tqhd,tkhd->thqk', grad_out.astype(jnp.float32), value_all.astype(jnp.float32))
    grad_scores = (attn_weights.astype(jnp.float32) * (grad_weights - row_inner)).astype(jnp.bfloat16)
    grad_qnorm = jnp.einsum('thqk,tkhd->tqhd', grad_scores.astype(jnp.float32), key_all.astype(jnp.float32)) * score_scale
    key_terms = jnp.einsum('thqk,tqhd->tkhd', grad_scores.astype(jnp.float32), q_norm.astype(jnp.float32)) * score_scale
    value_terms = jnp.einsum('thqk,tqhd->tkhd', attn_weights.astype(jnp.float32), grad_out.astype(jnp.float32))
    grad_knorm = gather_back(key_terms, tile_count)
    grad_vsum = gather_back(value_terms, tile_count)
    grad_queries = restore(grad_qnorm, q_unit, q_factor, q_gain).astype(jnp.bfloat16).reshape(-1, columns)
    grad_keys = restore(grad_knorm, k_unit, k_factor, k_gain).astype(jnp.bfloat16).reshape(-1, columns)
    grad_values = grad_vsum.astype(jnp.bfloat16).reshape(-1, columns)
    q_term = lax.optimization_barrier(jnp.sum(grad_qnorm * q_unit, axis=(0, 1, 2)))
    k_term = lax.optimization_barrier(jnp.sum(grad_knorm * k_unit, axis=(0, 1, 2)))
    return (attended.reshape(-1, columns), grad_queries, grad_keys, grad_values, q_term, k_term)

def reference(queries, keys, values, q_gain, k_gain, d_out, window):
    outputs = lax.map(lambda operands: one_sample(operands, q_gain, k_gain), (queries, keys, values, d_out, window))
    attended, grad_queries, grad_keys, grad_values, q_terms, k_terms = outputs
    pair_count = SAMPLES * HEADS
    return (attended, grad_queries, grad_keys, grad_values, lax.optimization_barrier(jnp.sum(q_terms, axis=0)) / pair_count, lax.optimization_barrier(jnp.sum(k_terms, axis=0)) / pair_count)
```

```python
import math

import jax
import jax.numpy as jnp
from jax import lax
from jax.sharding import PartitionSpec as P

EPSILON = 1e-06


def extended_2(cells, sides, width):
    for axis, dim in sides:
        count = lax.axis_size(axis)
        ends = count - 1
        head = lax.slice_in_dim(cells, 0, width, axis=dim)
        tail = lax.slice_in_dim(cells, cells.shape[dim] - width, cells.shape[dim], axis=dim)
        cells = jnp.concatenate(
            [
                lax.ppermute(tail, axis, [(i, (i + 1) % count) for i in range(ends)]),
                cells,
                lax.ppermute(head, axis, [((i + 1) % count, i) for i in range(ends)]),
            ],
            axis=dim,
        )
    return cells


def butterfly_sum(value, axes):
    for axis in axes:
        count = lax.axis_size(axis)
        step = 1
        while step < count:
            value = value + lax.ppermute(value, axis, [(i, i ^ step) for i in range(count)])
            step *= 2
    return value


def normalize(raw_rows, gain_vector):
    shaped = raw_rows.astype(jnp.float32).reshape(
        raw_rows.shape[0], raw_rows.shape[1], -1, gain_vector.shape[0]
    )
    factor = lax.rsqrt(jnp.mean(shaped * shaped, axis=-1, keepdims=True) + EPSILON)
    unit_rows = shaped * factor
    return (unit_rows, factor, (unit_rows * gain_vector).astype(jnp.bfloat16))


def restore(grad_norm, unit_rows, factor, gain_vector):
    scaled = grad_norm * gain_vector
    inner_mean = jnp.mean(scaled * unit_rows, axis=-1, keepdims=True)
    return factor * (scaled - unit_rows * inner_mean)


def head_pass(operands, allowed, score_scale):
    query_rows, key_rows, value_rows, grad_rows = operands
    scores = (
        jnp.einsum("sqd,skd->sqk", query_rows, key_rows, preferred_element_type=jnp.float32)
        * score_scale
    )
    scores = jnp.where(allowed[:, None, :], scores, -jnp.inf)
    row_max = jnp.max(scores, axis=-1, keepdims=True)
    row_sum = jnp.sum(jnp.exp(scores - row_max), axis=-1, keepdims=True)
    log_total = row_max + jnp.log(row_sum)
    attn_weights = jnp.exp(scores - log_total).astype(jnp.bfloat16)
    attended = jnp.einsum(
        "sqk,skd->sqd", attn_weights, value_rows, preferred_element_type=jnp.float32
    ).astype(jnp.bfloat16)
    row_inner = jnp.sum(
        grad_rows.astype(jnp.float32) * attended.astype(jnp.float32), axis=-1, keepdims=True
    )
    grad_weights = jnp.einsum(
        "sqd,skd->sqk", grad_rows, value_rows, preferred_element_type=jnp.float32
    )
    grad_scores = (attn_weights.astype(jnp.float32) * (grad_weights - row_inner)).astype(
        jnp.bfloat16
    )
    grad_query = (
        jnp.einsum("sqk,skd->sqd", grad_scores, key_rows, preferred_element_type=jnp.float32)
        * score_scale
    )
    return (attended, log_total[..., 0], row_inner[..., 0], grad_query, attn_weights, grad_scores)


def key_terms(grad_scores, attn_weights, query_norm, grad_out, score_scale):
    key_part = (
        jnp.einsum("hsqk,sqhd->skhd", grad_scores, query_norm, preferred_element_type=jnp.float32)
        * score_scale
    )
    value_part = jnp.einsum(
        "hsqk,sqhd->skhd", attn_weights, grad_out, preferred_element_type=jnp.float32
    )
    return (key_part, value_part)


def pack_terms(key_part, value_part):
    sample_count, tile_rows = (key_part.shape[0], key_part.shape[1])
    joined = jnp.concatenate(
        [
            key_part.reshape(sample_count, tile_rows, -1),
            value_part.reshape(sample_count, tile_rows, -1),
        ],
        axis=2,
    )
    return joined.astype(jnp.bfloat16)


def per_device(queries, keys, values, q_gain, k_gain, d_out, window):
    sample_count, tile_rows, columns = queries.shape
    head_size = q_gain.shape[0]
    head_count = columns // head_size
    score_scale = 1.0 / math.sqrt(head_size)
    q_unit, q_factor, q_norm = normalize(queries, q_gain)
    packed = jnp.concatenate([keys, values], axis=2)
    extended = extended_2(packed, (("seq", 1),), tile_rows)
    k_unit_all, k_factor_all, key_all = normalize(extended[..., :columns], k_gain)
    k_unit = k_unit_all[:, tile_rows : 2 * tile_rows]
    k_factor = k_factor_all[:, tile_rows : 2 * tile_rows]
    value_all = extended[..., columns:].reshape(sample_count, 3 * tile_rows, head_count, head_size)
    tile_index = lax.axis_index("seq")
    tile_count = lax.axis_size("seq")
    listing = window[:, 0, :]

    def listed(target):
        return jnp.any(listing == target, axis=-1) & (target >= 0) & (target < tile_count)

    left_ok = listed(tile_index - 1)
    right_ok = listed(tile_index + 1)
    block_flags = jnp.stack([left_ok, listed(tile_index), right_ok], axis=1)
    allowed = jnp.repeat(block_flags, tile_rows, axis=1)
    grad_out = d_out.reshape(sample_count, tile_rows, head_count, head_size)
    operands = (
        jnp.moveaxis(q_norm, 2, 0),
        jnp.moveaxis(key_all, 2, 0),
        jnp.moveaxis(value_all, 2, 0),
        jnp.moveaxis(grad_out, 2, 0),
    )
    results = lax.map(lambda per_head: head_pass(per_head, allowed, score_scale), operands)
    attended, log_total, row_inner, grad_query, attn_weights, grad_scores = results
    attended = jnp.moveaxis(attended, 0, 2).reshape(sample_count, tile_rows, columns)
    grad_qnorm = jnp.moveaxis(grad_query, 0, 2)
    key_every, value_every = key_terms(grad_scores, attn_weights, q_norm, grad_out, score_scale)
    left_terms = (key_every[:, :tile_rows], value_every[:, :tile_rows])
    own_terms = (key_every[:, tile_rows : 2 * tile_rows], value_every[:, tile_rows : 2 * tile_rows])
    right_terms = (key_every[:, 2 * tile_rows :], value_every[:, 2 * tile_rows :])
    outgoing = jnp.concatenate(
        [pack_terms(left_terms[0], left_terms[1]), pack_terms(right_terms[0], right_terms[1])],
        axis=1,
    )
    returned = extended_2(outgoing, (("seq", 1),), tile_rows)
    incoming = returned[:, :tile_rows].astype(jnp.float32) + returned[:, 3 * tile_rows :].astype(
        jnp.float32
    )
    grad_knorm = own_terms[0] + incoming[..., :columns].reshape(
        sample_count, tile_rows, head_count, head_size
    )
    grad_vsum = own_terms[1] + incoming[..., columns:].reshape(
        sample_count, tile_rows, head_count, head_size
    )
    grad_queries = (
        restore(grad_qnorm, q_unit, q_factor, q_gain)
        .astype(jnp.bfloat16)
        .reshape(sample_count, tile_rows, columns)
    )
    grad_keys = (
        restore(grad_knorm, k_unit, k_factor, k_gain)
        .astype(jnp.bfloat16)
        .reshape(sample_count, tile_rows, columns)
    )
    grad_values = grad_vsum.astype(jnp.bfloat16).reshape(sample_count, tile_rows, columns)
    near_terms = jnp.concatenate(
        [
            left_terms[0].astype(jnp.bfloat16).astype(jnp.float32),
            own_terms[0],
            right_terms[0].astype(jnp.bfloat16).astype(jnp.float32),
        ],
        axis=1,
    )
    gain_terms = jnp.concatenate(
        [
            jnp.sum(grad_qnorm * q_unit, axis=(0, 1, 2)),
            jnp.sum(near_terms * k_unit_all, axis=(0, 1, 2)),
        ]
    )
    gain_totals = butterfly_sum(gain_terms, ("seq", "head", "fsdp"))
    q_total, k_total = gain_totals[:head_size], gain_totals[head_size:]
    pair_count = sample_count * lax.axis_size("fsdp") * head_count * lax.axis_size("head")
    return (
        attended,
        grad_queries,
        grad_keys,
        grad_values,
        q_total / pair_count,
        k_total / pair_count,
    )


def solution(mesh):
    return jax.shard_map(
        per_device,
        mesh=mesh,
        in_specs=(
            P("fsdp", "seq", "head"),
            P("fsdp", "seq", "head"),
            P("fsdp", "seq", "head"),
            P(),
            P(),
            P("fsdp", "seq", "head"),
            P("fsdp", "seq", None),
        ),
        out_specs=(
            P("fsdp", "seq", "head"),
            P("fsdp", "seq", "head"),
            P("fsdp", "seq", "head"),
            P("fsdp", "seq", "head"),
            P(),
            P(),
        ),
        check_vma=False,
    )
```

```python
import math

import jax
import jax.numpy as jnp
from jax import lax
from jax.sharding import PartitionSpec as P

EPSILON = 1e-06


def extended_2(cells, sides, width):
    for axis, dim in sides:
        count = lax.axis_size(axis)
        ends = count - 1
        head = lax.slice_in_dim(cells, 0, width, axis=dim)
        tail = lax.slice_in_dim(cells, cells.shape[dim] - width, cells.shape[dim], axis=dim)
        cells = jnp.concatenate(
            [
                lax.ppermute(tail, axis, [(i, (i + 1) % count) for i in range(ends)]),
                cells,
                lax.ppermute(head, axis, [((i + 1) % count, i) for i in range(ends)]),
            ],
            axis=dim,
        )
    return cells


def butterfly_sum(value, axes):
    for axis in axes:
        count = lax.axis_size(axis)
        step = 1
        while step < count:
            value = value + lax.ppermute(value, axis, [(i, i ^ step) for i in range(count)])
            step *= 2
    return value


def normalize(raw_rows, gain_vector):
    shaped = raw_rows.astype(jnp.float32).reshape(
        raw_rows.shape[0], raw_rows.shape[1], -1, gain_vector.shape[0]
    )
    factor = lax.rsqrt(jnp.mean(shaped * shaped, axis=-1, keepdims=True) + EPSILON)
    unit_rows = shaped * factor
    return (unit_rows, factor, (unit_rows * gain_vector).astype(jnp.bfloat16))


def restore(grad_norm, unit_rows, factor, gain_vector):
    scaled = grad_norm * gain_vector
    inner_mean = jnp.mean(scaled * unit_rows, axis=-1, keepdims=True)
    return factor * (scaled - unit_rows * inner_mean)


def head_pass(operands, allowed, score_scale):
    query_rows, key_rows, value_rows, grad_rows = operands
    scores = (
        jnp.einsum("sqd,skd->sqk", query_rows, key_rows, preferred_element_type=jnp.float32)
        * score_scale
    )
    scores = jnp.where(allowed[:, None, :], scores, -jnp.inf)
    row_max = jnp.max(scores, axis=-1, keepdims=True)
    row_sum = jnp.sum(jnp.exp(scores - row_max), axis=-1, keepdims=True)
    log_total = row_max + jnp.log(row_sum)
    attn_weights = jnp.exp(scores - log_total).astype(jnp.bfloat16)
    attended = jnp.einsum(
        "sqk,skd->sqd", attn_weights, value_rows, preferred_element_type=jnp.float32
    ).astype(jnp.bfloat16)
    row_inner = jnp.sum(
        grad_rows.astype(jnp.float32) * attended.astype(jnp.float32), axis=-1, keepdims=True
    )
    grad_weights = jnp.einsum(
        "sqd,skd->sqk", grad_rows, value_rows, preferred_element_type=jnp.float32
    )
    grad_scores = (attn_weights.astype(jnp.float32) * (grad_weights - row_inner)).astype(
        jnp.bfloat16
    )
    grad_query = (
        jnp.einsum("sqk,skd->sqd", grad_scores, key_rows, preferred_element_type=jnp.float32)
        * score_scale
    )
    return (attended, log_total[..., 0], row_inner[..., 0], grad_query, attn_weights, grad_scores)


def key_terms(grad_scores, attn_weights, query_norm, grad_out, score_scale):
    key_part = (
        jnp.einsum("hsqk,sqhd->skhd", grad_scores, query_norm, preferred_element_type=jnp.float32)
        * score_scale
    )
    value_part = jnp.einsum(
        "hsqk,sqhd->skhd", attn_weights, grad_out, preferred_element_type=jnp.float32
    )
    return (key_part, value_part)


def pack_terms(key_part, value_part):
    sample_count, tile_rows = (key_part.shape[0], key_part.shape[1])
    joined = jnp.concatenate(
        [
            key_part.reshape(sample_count, tile_rows, -1),
            value_part.reshape(sample_count, tile_rows, -1),
        ],
        axis=2,
    )
    return joined.astype(jnp.bfloat16)


def per_device(queries, keys, values, q_gain, k_gain, d_out, window):
    sample_count, tile_rows, columns = queries.shape
    head_size = q_gain.shape[0]
    head_count = columns // head_size
    score_scale = 1.0 / math.sqrt(head_size)
    q_unit, q_factor, q_norm = normalize(queries, q_gain)
    packed = jnp.concatenate([keys, values], axis=2)
    extended = extended_2(packed, (("seq", 1),), tile_rows)
    k_unit_all, k_factor_all, key_all = normalize(extended[..., :columns], k_gain)
    k_unit = k_unit_all[:, tile_rows : 2 * tile_rows]
    k_factor = k_factor_all[:, tile_rows : 2 * tile_rows]
    value_all = extended[..., columns:].reshape(sample_count, 3 * tile_rows, head_count, head_size)
    tile_index = lax.axis_index("seq")
    tile_count = lax.axis_size("seq")
    listing = window[:, 0, :]

    def listed(target):
        return jnp.any(listing == target, axis=-1) & (target >= 0) & (target < tile_count)

    left_ok = listed(tile_index - 1)
    right_ok = listed(tile_index + 1)
    block_flags = jnp.stack([left_ok, listed(tile_index), right_ok], axis=1)
    allowed = jnp.repeat(block_flags, tile_rows, axis=1)
    grad_out = d_out.reshape(sample_count, tile_rows, head_count, head_size)
    operands = (
        jnp.moveaxis(q_norm, 2, 0),
        jnp.moveaxis(key_all, 2, 0),
        jnp.moveaxis(value_all, 2, 0),
        jnp.moveaxis(grad_out, 2, 0),
    )
    results = jax.vmap(lambda per_head: head_pass(per_head, allowed, score_scale))(operands)
    attended, log_total, row_inner, grad_query, attn_weights, grad_scores = results
    attended = jnp.moveaxis(attended, 0, 2).reshape(sample_count, tile_rows, columns)
    grad_qnorm = jnp.moveaxis(grad_query, 0, 2)
    key_every, value_every = key_terms(grad_scores, attn_weights, q_norm, grad_out, score_scale)
    left_terms = (key_every[:, :tile_rows], value_every[:, :tile_rows])
    own_terms = (key_every[:, tile_rows : 2 * tile_rows], value_every[:, tile_rows : 2 * tile_rows])
    right_terms = (key_every[:, 2 * tile_rows :], value_every[:, 2 * tile_rows :])
    outgoing = jnp.concatenate(
        [pack_terms(left_terms[0], left_terms[1]), pack_terms(right_terms[0], right_terms[1])],
        axis=1,
    )
    returned = extended_2(outgoing, (("seq", 1),), tile_rows)
    incoming = returned[:, :tile_rows].astype(jnp.float32) + returned[:, 3 * tile_rows :].astype(
        jnp.float32
    )
    grad_knorm = own_terms[0] + incoming[..., :columns].reshape(
        sample_count, tile_rows, head_count, head_size
    )
    grad_vsum = own_terms[1] + incoming[..., columns:].reshape(
        sample_count, tile_rows, head_count, head_size
    )
    grad_queries = (
        restore(grad_qnorm, q_unit, q_factor, q_gain)
        .astype(jnp.bfloat16)
        .reshape(sample_count, tile_rows, columns)
    )
    grad_keys = (
        restore(grad_knorm, k_unit, k_factor, k_gain)
        .astype(jnp.bfloat16)
        .reshape(sample_count, tile_rows, columns)
    )
    grad_values = grad_vsum.astype(jnp.bfloat16).reshape(sample_count, tile_rows, columns)
    near_terms = jnp.concatenate(
        [
            left_terms[0].astype(jnp.bfloat16).astype(jnp.float32),
            own_terms[0],
            right_terms[0].astype(jnp.bfloat16).astype(jnp.float32),
        ],
        axis=1,
    )
    gain_terms = jnp.concatenate(
        [
            jnp.sum(grad_qnorm * q_unit, axis=(0, 1, 2)),
            jnp.sum(near_terms * k_unit_all, axis=(0, 1, 2)),
        ]
    )
    gain_totals = butterfly_sum(gain_terms, ("seq", "head", "fsdp"))
    q_total, k_total = gain_totals[:head_size], gain_totals[head_size:]
    pair_count = sample_count * lax.axis_size("fsdp") * head_count * lax.axis_size("head")
    return (
        attended,
        grad_queries,
        grad_keys,
        grad_values,
        q_total / pair_count,
        k_total / pair_count,
    )


def solution(mesh):
    return jax.shard_map(
        per_device,
        mesh=mesh,
        in_specs=(
            P("fsdp", "seq", "head"),
            P("fsdp", "seq", "head"),
            P("fsdp", "seq", "head"),
            P(),
            P(),
            P("fsdp", "seq", "head"),
            P("fsdp", "seq", None),
        ),
        out_specs=(
            P("fsdp", "seq", "head"),
            P("fsdp", "seq", "head"),
            P("fsdp", "seq", "head"),
            P("fsdp", "seq", "head"),
            P(),
            P(),
        ),
        check_vma=False,
    )
```

```python
import math

import jax
import jax.numpy as jnp
from jax import lax
from jax.sharding import PartitionSpec as P

EPSILON = 1e-06


def extended_2(cells, sides, width):
    for axis, dim in sides:
        count = lax.axis_size(axis)
        ends = count - 1
        head = lax.slice_in_dim(cells, 0, width, axis=dim)
        tail = lax.slice_in_dim(cells, cells.shape[dim] - width, cells.shape[dim], axis=dim)
        cells = jnp.concatenate(
            [
                lax.ppermute(tail, axis, [(i, (i + 1) % count) for i in range(ends)]),
                cells,
                lax.ppermute(head, axis, [((i + 1) % count, i) for i in range(ends)]),
            ],
            axis=dim,
        )
    return cells


def butterfly_sum(value, axes):
    for axis in axes:
        count = lax.axis_size(axis)
        step = 1
        while step < count:
            value = value + lax.ppermute(value, axis, [(i, i ^ step) for i in range(count)])
            step *= 2
    return value


def normalize(raw_rows, gain_vector):
    shaped = raw_rows.astype(jnp.float32).reshape(
        raw_rows.shape[0], raw_rows.shape[1], -1, gain_vector.shape[0]
    )
    factor = lax.rsqrt(jnp.mean(shaped * shaped, axis=-1, keepdims=True) + EPSILON)
    unit_rows = shaped * factor
    return (unit_rows, factor, (unit_rows * gain_vector).astype(jnp.bfloat16))


def restore(grad_norm, unit_rows, factor, gain_vector):
    scaled = grad_norm * gain_vector
    inner_mean = jnp.mean(scaled * unit_rows, axis=-1, keepdims=True)
    return factor * (scaled - unit_rows * inner_mean)


def head_pass(operands, allowed, score_scale):
    query_rows, key_rows, value_rows, grad_rows = operands
    scores = (
        jnp.einsum("sqd,skd->sqk", query_rows, key_rows, preferred_element_type=jnp.float32)
        * score_scale
    )
    scores = jnp.where(allowed[:, None, :], scores, -jnp.inf)
    row_max = jnp.max(scores, axis=-1, keepdims=True)
    row_sum = jnp.sum(jnp.exp(scores - row_max), axis=-1, keepdims=True)
    log_total = row_max + jnp.log(row_sum)
    attn_weights = jnp.exp(scores - log_total).astype(jnp.bfloat16)
    attended = jnp.einsum(
        "sqk,skd->sqd", attn_weights, value_rows, preferred_element_type=jnp.float32
    ).astype(jnp.bfloat16)
    row_inner = jnp.sum(
        grad_rows.astype(jnp.float32) * attended.astype(jnp.float32), axis=-1, keepdims=True
    )
    grad_weights = jnp.einsum(
        "sqd,skd->sqk", grad_rows, value_rows, preferred_element_type=jnp.float32
    )
    grad_scores = (attn_weights.astype(jnp.float32) * (grad_weights - row_inner)).astype(
        jnp.bfloat16
    )
    grad_query = (
        jnp.einsum("sqk,skd->sqd", grad_scores, key_rows, preferred_element_type=jnp.float32)
        * score_scale
    )
    return (attended, log_total[..., 0], row_inner[..., 0], grad_query, attn_weights, grad_scores)


def key_terms(grad_scores, attn_weights, query_norm, grad_out, score_scale):
    key_part = (
        jnp.einsum("hsqk,sqhd->skhd", grad_scores, query_norm, preferred_element_type=jnp.float32)
        * score_scale
    )
    value_part = jnp.einsum(
        "hsqk,sqhd->skhd", attn_weights, grad_out, preferred_element_type=jnp.float32
    )
    return (key_part, value_part)


def pack_terms(key_part, value_part):
    sample_count, tile_rows = (key_part.shape[0], key_part.shape[1])
    joined = jnp.concatenate(
        [
            key_part.reshape(sample_count, tile_rows, -1),
            value_part.reshape(sample_count, tile_rows, -1),
        ],
        axis=2,
    )
    return joined.astype(jnp.bfloat16)


def per_device(queries, keys, values, q_gain, k_gain, d_out, window):
    sample_count, tile_rows, columns = queries.shape
    head_size = q_gain.shape[0]
    head_count = columns // head_size
    score_scale = 1.0 / math.sqrt(head_size)
    q_unit, q_factor, q_norm = normalize(queries, q_gain)
    packed = jnp.concatenate([keys, values], axis=2)
    extended = extended_2(packed, (("seq", 1),), tile_rows)
    k_unit_all, k_factor_all, key_all = normalize(extended[..., :columns], k_gain)
    k_unit = k_unit_all[:, tile_rows : 2 * tile_rows]
    k_factor = k_factor_all[:, tile_rows : 2 * tile_rows]
    value_all = extended[..., columns:].reshape(sample_count, 3 * tile_rows, head_count, head_size)
    tile_index = lax.axis_index("seq")
    tile_count = lax.axis_size("seq")
    listing = window[:, 0, :]

    def listed(target):
        return jnp.any(listing == target, axis=-1) & (target >= 0) & (target < tile_count)

    left_ok = listed(tile_index - 1)
    right_ok = listed(tile_index + 1)
    block_flags = jnp.stack([left_ok, listed(tile_index), right_ok], axis=1)
    allowed = jnp.repeat(block_flags, tile_rows, axis=1)
    grad_out = d_out.reshape(sample_count, tile_rows, head_count, head_size)
    operands = (
        jnp.moveaxis(q_norm, 2, 0),
        jnp.moveaxis(key_all, 2, 0),
        jnp.moveaxis(value_all, 2, 0),
        jnp.moveaxis(grad_out, 2, 0),
    )
    results = jax.vmap(lambda per_head: head_pass(per_head, allowed, score_scale))(operands)
    attended, log_total, row_inner, grad_query, attn_weights, grad_scores = results
    attended = jnp.moveaxis(attended, 0, 2).reshape(sample_count, tile_rows, columns)
    grad_qnorm = jnp.moveaxis(grad_query, 0, 2)
    key_every, value_every = key_terms(grad_scores, attn_weights, q_norm, grad_out, score_scale)
    left_terms = (key_every[:, :tile_rows], value_every[:, :tile_rows])
    own_terms = (key_every[:, tile_rows : 2 * tile_rows], value_every[:, tile_rows : 2 * tile_rows])
    right_terms = (key_every[:, 2 * tile_rows :], value_every[:, 2 * tile_rows :])
    outgoing = jnp.concatenate(
        [pack_terms(left_terms[0], left_terms[1]), pack_terms(right_terms[0], right_terms[1])],
        axis=1,
    )
    grad_queries = (
        restore(grad_qnorm, q_unit, q_factor, q_gain)
        .astype(jnp.bfloat16)
        .reshape(sample_count, tile_rows, columns)
    )
    near_terms = jnp.concatenate(
        [
            left_terms[0].astype(jnp.bfloat16).astype(jnp.float32),
            own_terms[0],
            right_terms[0].astype(jnp.bfloat16).astype(jnp.float32),
        ],
        axis=1,
    )
    gain_terms = jnp.concatenate(
        [
            jnp.sum(grad_qnorm * q_unit, axis=(0, 1, 2)),
            jnp.sum(near_terms * k_unit_all, axis=(0, 1, 2)),
        ]
    )
    gain_totals = butterfly_sum(gain_terms, ("seq", "head", "fsdp"))
    returned = extended_2(outgoing, (("seq", 1),), tile_rows)
    returned, gain_totals = lax.optimization_barrier((returned, gain_totals))
    incoming = returned[:, :tile_rows].astype(jnp.float32) + returned[:, 3 * tile_rows :].astype(
        jnp.float32
    )
    grad_knorm = own_terms[0] + incoming[..., :columns].reshape(
        sample_count, tile_rows, head_count, head_size
    )
    grad_vsum = own_terms[1] + incoming[..., columns:].reshape(
        sample_count, tile_rows, head_count, head_size
    )
    grad_keys = (
        restore(grad_knorm, k_unit, k_factor, k_gain)
        .astype(jnp.bfloat16)
        .reshape(sample_count, tile_rows, columns)
    )
    grad_values = grad_vsum.astype(jnp.bfloat16).reshape(sample_count, tile_rows, columns)
    q_total, k_total = gain_totals[:head_size], gain_totals[head_size:]
    pair_count = sample_count * lax.axis_size("fsdp") * head_count * lax.axis_size("head")
    return (
        attended,
        grad_queries,
        grad_keys,
        grad_values,
        q_total / pair_count,
        k_total / pair_count,
    )


def solution(mesh):
    return jax.shard_map(
        per_device,
        mesh=mesh,
        in_specs=(
            P("fsdp", "seq", "head"),
            P("fsdp", "seq", "head"),
            P("fsdp", "seq", "head"),
            P(),
            P(),
            P("fsdp", "seq", "head"),
            P("fsdp", "seq", None),
        ),
        out_specs=(
            P("fsdp", "seq", "head"),
            P("fsdp", "seq", "head"),
            P("fsdp", "seq", "head"),
            P("fsdp", "seq", "head"),
            P(),
            P(),
        ),
        check_vma=False,
    )
```

```python
import math

import jax
import jax.numpy as jnp
from jax import lax
from jax.sharding import PartitionSpec as P

EPSILON = 1e-06


def extended_2(cells, sides, width):
    for axis, dim in sides:
        count = lax.axis_size(axis)
        ends = count - 1
        head = lax.slice_in_dim(cells, 0, width, axis=dim)
        tail = lax.slice_in_dim(cells, cells.shape[dim] - width, cells.shape[dim], axis=dim)
        cells = jnp.concatenate(
            [
                lax.ppermute(tail, axis, [(i, (i + 1) % count) for i in range(ends)]),
                cells,
                lax.ppermute(head, axis, [((i + 1) % count, i) for i in range(ends)]),
            ],
            axis=dim,
        )
    return cells


def butterfly_sum(value, axes):
    for axis in axes:
        count = lax.axis_size(axis)
        step = 1
        while step < count:
            value = value + lax.ppermute(value, axis, [(i, i ^ step) for i in range(count)])
            step *= 2
    return value


def normalize(raw_rows, gain_vector):
    shaped = raw_rows.astype(jnp.float32).reshape(
        raw_rows.shape[0], raw_rows.shape[1], -1, gain_vector.shape[0]
    )
    factor = lax.rsqrt(jnp.mean(shaped * shaped, axis=-1, keepdims=True) + EPSILON)
    unit_rows = shaped * factor
    return (unit_rows, factor, (unit_rows * gain_vector).astype(jnp.bfloat16))


def restore(grad_norm, unit_rows, factor, gain_vector):
    scaled = grad_norm * gain_vector
    inner_mean = jnp.mean(scaled * unit_rows, axis=-1, keepdims=True)
    return factor * (scaled - unit_rows * inner_mean)


def head_pass(operands, allowed, score_scale):
    query_rows, key_rows, value_rows, grad_rows = operands
    scores = (
        jnp.einsum("sqd,skd->sqk", query_rows, key_rows, preferred_element_type=jnp.float32)
        * score_scale
    )
    scores = jnp.where(allowed[:, None, :], scores, -jnp.inf)
    row_max = jnp.max(scores, axis=-1, keepdims=True)
    row_sum = jnp.sum(jnp.exp(scores - row_max), axis=-1, keepdims=True)
    log_total = row_max + jnp.log(row_sum)
    attn_weights = jnp.exp(scores - log_total).astype(jnp.bfloat16)
    attended = jnp.einsum(
        "sqk,skd->sqd", attn_weights, value_rows, preferred_element_type=jnp.float32
    ).astype(jnp.bfloat16)
    row_inner = jnp.sum(
        grad_rows.astype(jnp.float32) * attended.astype(jnp.float32), axis=-1, keepdims=True
    )
    grad_weights = jnp.einsum(
        "sqd,skd->sqk", grad_rows, value_rows, preferred_element_type=jnp.float32
    )
    grad_scores = (attn_weights.astype(jnp.float32) * (grad_weights - row_inner)).astype(
        jnp.bfloat16
    )
    grad_query = (
        jnp.einsum("sqk,skd->sqd", grad_scores, key_rows, preferred_element_type=jnp.float32)
        * score_scale
    )
    return (attended, log_total[..., 0], row_inner[..., 0], grad_query, attn_weights, grad_scores)


def key_terms(grad_scores, attn_weights, query_norm, grad_out, score_scale):
    key_part = (
        jnp.einsum("hsqk,sqhd->skhd", grad_scores, query_norm, preferred_element_type=jnp.float32)
        * score_scale
    )
    value_part = jnp.einsum(
        "hsqk,sqhd->skhd", attn_weights, grad_out, preferred_element_type=jnp.float32
    )
    return (key_part, value_part)


def pack_terms(key_part, value_part):
    sample_count, tile_rows = (key_part.shape[0], key_part.shape[1])
    joined = jnp.concatenate(
        [
            key_part.reshape(sample_count, tile_rows, -1),
            value_part.reshape(sample_count, tile_rows, -1),
        ],
        axis=2,
    )
    return joined.astype(jnp.bfloat16)


def per_device(queries, keys, values, q_gain, k_gain, d_out, window):
    sample_count, tile_rows, columns = queries.shape
    head_size = q_gain.shape[0]
    head_count = columns // head_size
    score_scale = 1.0 / math.sqrt(head_size)
    q_unit, q_factor, q_norm = normalize(queries, q_gain)
    packed = jnp.concatenate([keys, values], axis=2)
    extended = extended_2(packed, (("seq", 1),), tile_rows)
    k_unit_all, k_factor_all, key_all = normalize(extended[..., :columns], k_gain)
    k_unit = k_unit_all[:, tile_rows : 2 * tile_rows]
    k_factor = k_factor_all[:, tile_rows : 2 * tile_rows]
    value_all = extended[..., columns:].reshape(sample_count, 3 * tile_rows, head_count, head_size)
    tile_index = lax.axis_index("seq")
    tile_count = lax.axis_size("seq")
    listing = window[:, 0, :]

    def listed(target):
        return jnp.any(listing == target, axis=-1) & (target >= 0) & (target < tile_count)

    left_ok = listed(tile_index - 1)
    right_ok = listed(tile_index + 1)
    block_flags = jnp.stack([left_ok, listed(tile_index), right_ok], axis=1)
    allowed = jnp.repeat(block_flags, tile_rows, axis=1)
    grad_out = d_out.reshape(sample_count, tile_rows, head_count, head_size)
    operands = (
        jnp.moveaxis(q_norm, 2, 0),
        jnp.moveaxis(key_all, 2, 0),
        jnp.moveaxis(value_all, 2, 0),
        jnp.moveaxis(grad_out, 2, 0),
    )
    results = jax.vmap(lambda per_head: head_pass(per_head, allowed, score_scale))(operands)
    attended, log_total, row_inner, grad_query, attn_weights, grad_scores = results
    attended = jnp.moveaxis(attended, 0, 2).reshape(sample_count, tile_rows, columns)
    grad_qnorm = jnp.moveaxis(grad_query, 0, 2)
    key_every, value_every = key_terms(grad_scores, attn_weights, q_norm, grad_out, score_scale)
    left_terms = (key_every[:, :tile_rows], value_every[:, :tile_rows])
    own_terms = (key_every[:, tile_rows : 2 * tile_rows], value_every[:, tile_rows : 2 * tile_rows])
    right_terms = (key_every[:, 2 * tile_rows :], value_every[:, 2 * tile_rows :])
    grad_queries = (
        restore(grad_qnorm, q_unit, q_factor, q_gain)
        .astype(jnp.bfloat16)
        .reshape(sample_count, tile_rows, columns)
    )
    near_terms = jnp.concatenate(
        [
            left_terms[0].astype(jnp.bfloat16).astype(jnp.float32),
            own_terms[0],
            right_terms[0].astype(jnp.bfloat16).astype(jnp.float32),
        ],
        axis=1,
    )
    gain_terms = jnp.concatenate(
        [
            jnp.sum(grad_qnorm * q_unit, axis=(0, 1, 2)),
            jnp.sum(near_terms * k_unit_all, axis=(0, 1, 2)),
        ]
    )
    gain_totals = butterfly_sum(gain_terms, ("seq", "head", "fsdp"))
    ends = tile_count - 1
    from_left = lax.ppermute(
        pack_terms(right_terms[0], right_terms[1]), "seq", [(i, i + 1) for i in range(ends)]
    )
    from_right = lax.ppermute(
        pack_terms(left_terms[0], left_terms[1]), "seq", [(i + 1, i) for i in range(ends)]
    )
    from_left, from_right, gain_totals = lax.optimization_barrier(
        (from_left, from_right, gain_totals)
    )
    incoming = from_left.astype(jnp.float32) + from_right.astype(jnp.float32)
    grad_knorm = own_terms[0] + incoming[..., :columns].reshape(
        sample_count, tile_rows, head_count, head_size
    )
    grad_vsum = own_terms[1] + incoming[..., columns:].reshape(
        sample_count, tile_rows, head_count, head_size
    )
    grad_keys = (
        restore(grad_knorm, k_unit, k_factor, k_gain)
        .astype(jnp.bfloat16)
        .reshape(sample_count, tile_rows, columns)
    )
    grad_values = grad_vsum.astype(jnp.bfloat16).reshape(sample_count, tile_rows, columns)
    q_total, k_total = gain_totals[:head_size], gain_totals[head_size:]
    pair_count = sample_count * lax.axis_size("fsdp") * head_count * lax.axis_size("head")
    return (
        attended,
        grad_queries,
        grad_keys,
        grad_values,
        q_total / pair_count,
        k_total / pair_count,
    )


def solution(mesh):
    return jax.shard_map(
        per_device,
        mesh=mesh,
        in_specs=(
            P("fsdp", "seq", "head"),
            P("fsdp", "seq", "head"),
            P("fsdp", "seq", "head"),
            P(),
            P(),
            P("fsdp", "seq", "head"),
            P("fsdp", "seq", None),
        ),
        out_specs=(
            P("fsdp", "seq", "head"),
            P("fsdp", "seq", "head"),
            P("fsdp", "seq", "head"),
            P("fsdp", "seq", "head"),
            P(),
            P(),
        ),
        check_vma=False,
    )
```

```python
import math

import jax
import jax.numpy as jnp
from jax import lax
from jax.sharding import PartitionSpec as P

EPSILON = 1e-06


def extended_2(cells, sides, width):
    for axis, dim in sides:
        count = lax.axis_size(axis)
        ends = count - 1
        head = lax.slice_in_dim(cells, 0, width, axis=dim)
        tail = lax.slice_in_dim(cells, cells.shape[dim] - width, cells.shape[dim], axis=dim)
        cells = jnp.concatenate(
            [
                lax.ppermute(tail, axis, [(i, (i + 1) % count) for i in range(ends)]),
                cells,
                lax.ppermute(head, axis, [((i + 1) % count, i) for i in range(ends)]),
            ],
            axis=dim,
        )
    return cells


def butterfly_sum(value, stages):
    for axes, mask in stages:
        count = math.prod(lax.axis_size(axis) for axis in axes)
        value = value + lax.ppermute(value, axes, [(i, i ^ mask) for i in range(count)])
    return value


def gain_stages():
    seq_count = lax.axis_size("seq")
    head_count = lax.axis_size("head")
    fsdp_count = lax.axis_size("fsdp")
    stages = []
    step = 1
    while step < seq_count:
        stages.append((("seq",), step))
        step *= 2
    stages.append((("head",), 1))
    half = seq_count // 2
    step = 2
    while step < head_count:
        stages.append((("seq", "head"), half * head_count + step))
        step *= 2
    side = math.isqrt(fsdp_count)
    for base in (1, side):
        stages.append((("fsdp",), base))
        stages.append((("fsdp",), 3 * base))
    return stages


def normalize(raw_rows, gain_vector):
    shaped = raw_rows.astype(jnp.float32).reshape(
        raw_rows.shape[0], raw_rows.shape[1], -1, gain_vector.shape[0]
    )
    factor = lax.rsqrt(jnp.mean(shaped * shaped, axis=-1, keepdims=True) + EPSILON)
    unit_rows = shaped * factor
    return (unit_rows, factor, (unit_rows * gain_vector).astype(jnp.bfloat16))


def restore(grad_norm, unit_rows, factor, gain_vector):
    scaled = grad_norm * gain_vector
    inner_mean = jnp.mean(scaled * unit_rows, axis=-1, keepdims=True)
    return factor * (scaled - unit_rows * inner_mean)


def head_pass(operands, allowed, score_scale):
    query_rows, key_rows, value_rows, grad_rows = operands
    scores = (
        jnp.einsum("sqd,skd->sqk", query_rows, key_rows, preferred_element_type=jnp.float32)
        * score_scale
    )
    scores = jnp.where(allowed[:, None, :], scores, -jnp.inf)
    row_max = jnp.max(scores, axis=-1, keepdims=True)
    row_sum = jnp.sum(jnp.exp(scores - row_max), axis=-1, keepdims=True)
    log_total = row_max + jnp.log(row_sum)
    attn_weights = jnp.exp(scores - log_total).astype(jnp.bfloat16)
    attended = jnp.einsum(
        "sqk,skd->sqd", attn_weights, value_rows, preferred_element_type=jnp.float32
    ).astype(jnp.bfloat16)
    row_inner = jnp.sum(
        grad_rows.astype(jnp.float32) * attended.astype(jnp.float32), axis=-1, keepdims=True
    )
    grad_weights = jnp.einsum(
        "sqd,skd->sqk", grad_rows, value_rows, preferred_element_type=jnp.float32
    )
    grad_scores = (attn_weights.astype(jnp.float32) * (grad_weights - row_inner)).astype(
        jnp.bfloat16
    )
    grad_query = (
        jnp.einsum("sqk,skd->sqd", grad_scores, key_rows, preferred_element_type=jnp.float32)
        * score_scale
    )
    return (attended, log_total[..., 0], row_inner[..., 0], grad_query, attn_weights, grad_scores)


def key_terms(grad_scores, attn_weights, query_norm, grad_out, score_scale):
    key_part = (
        jnp.einsum("hsqk,sqhd->skhd", grad_scores, query_norm, preferred_element_type=jnp.float32)
        * score_scale
    )
    value_part = jnp.einsum(
        "hsqk,sqhd->skhd", attn_weights, grad_out, preferred_element_type=jnp.float32
    )
    return (key_part, value_part)


def pack_terms(key_part, value_part):
    sample_count, tile_rows = (key_part.shape[0], key_part.shape[1])
    joined = jnp.concatenate(
        [
            key_part.reshape(sample_count, tile_rows, -1),
            value_part.reshape(sample_count, tile_rows, -1),
        ],
        axis=2,
    )
    return joined.astype(jnp.bfloat16)


def per_device(queries, keys, values, q_gain, k_gain, d_out, window):
    sample_count, tile_rows, columns = queries.shape
    head_size = q_gain.shape[0]
    head_count = columns // head_size
    score_scale = 1.0 / math.sqrt(head_size)
    q_unit, q_factor, q_norm = normalize(queries, q_gain)
    packed = jnp.concatenate([keys, values], axis=2)
    extended = extended_2(packed, (("seq", 1),), tile_rows)
    k_unit_all, k_factor_all, key_all = normalize(extended[..., :columns], k_gain)
    k_unit = k_unit_all[:, tile_rows : 2 * tile_rows]
    k_factor = k_factor_all[:, tile_rows : 2 * tile_rows]
    value_all = extended[..., columns:].reshape(sample_count, 3 * tile_rows, head_count, head_size)
    tile_index = lax.axis_index("seq")
    tile_count = lax.axis_size("seq")
    listing = window[:, 0, :]

    def listed(target):
        return jnp.any(listing == target, axis=-1) & (target >= 0) & (target < tile_count)

    left_ok = listed(tile_index - 1)
    right_ok = listed(tile_index + 1)
    block_flags = jnp.stack([left_ok, listed(tile_index), right_ok], axis=1)
    allowed = jnp.repeat(block_flags, tile_rows, axis=1)
    grad_out = d_out.reshape(sample_count, tile_rows, head_count, head_size)
    operands = (
        jnp.moveaxis(q_norm, 2, 0),
        jnp.moveaxis(key_all, 2, 0),
        jnp.moveaxis(value_all, 2, 0),
        jnp.moveaxis(grad_out, 2, 0),
    )
    results = jax.vmap(lambda per_head: head_pass(per_head, allowed, score_scale))(operands)
    attended, log_total, row_inner, grad_query, attn_weights, grad_scores = results
    attended = jnp.moveaxis(attended, 0, 2).reshape(sample_count, tile_rows, columns)
    grad_qnorm = jnp.moveaxis(grad_query, 0, 2)
    key_every, value_every = key_terms(grad_scores, attn_weights, q_norm, grad_out, score_scale)
    left_terms = (key_every[:, :tile_rows], value_every[:, :tile_rows])
    own_terms = (key_every[:, tile_rows : 2 * tile_rows], value_every[:, tile_rows : 2 * tile_rows])
    right_terms = (key_every[:, 2 * tile_rows :], value_every[:, 2 * tile_rows :])
    grad_queries = (
        restore(grad_qnorm, q_unit, q_factor, q_gain)
        .astype(jnp.bfloat16)
        .reshape(sample_count, tile_rows, columns)
    )
    near_terms = jnp.concatenate(
        [
            left_terms[0].astype(jnp.bfloat16).astype(jnp.float32),
            own_terms[0],
            right_terms[0].astype(jnp.bfloat16).astype(jnp.float32),
        ],
        axis=1,
    )
    gain_terms = jnp.concatenate(
        [
            jnp.sum(grad_qnorm * q_unit, axis=(0, 1, 2)),
            jnp.sum(near_terms * k_unit_all, axis=(0, 1, 2)),
        ]
    )
    gain_totals = butterfly_sum(gain_terms, gain_stages())
    ends = tile_count - 1
    from_left = lax.ppermute(
        pack_terms(right_terms[0], right_terms[1]), "seq", [(i, i + 1) for i in range(ends)]
    )
    from_right = lax.ppermute(
        pack_terms(left_terms[0], left_terms[1]), "seq", [(i + 1, i) for i in range(ends)]
    )
    from_left, from_right, gain_totals = lax.optimization_barrier(
        (from_left, from_right, gain_totals)
    )
    incoming = from_left.astype(jnp.float32) + from_right.astype(jnp.float32)
    grad_knorm = own_terms[0] + incoming[..., :columns].reshape(
        sample_count, tile_rows, head_count, head_size
    )
    grad_vsum = own_terms[1] + incoming[..., columns:].reshape(
        sample_count, tile_rows, head_count, head_size
    )
    grad_keys = (
        restore(grad_knorm, k_unit, k_factor, k_gain)
        .astype(jnp.bfloat16)
        .reshape(sample_count, tile_rows, columns)
    )
    grad_values = grad_vsum.astype(jnp.bfloat16).reshape(sample_count, tile_rows, columns)
    q_total, k_total = gain_totals[:head_size], gain_totals[head_size:]
    pair_count = sample_count * lax.axis_size("fsdp") * head_count * lax.axis_size("head")
    return (
        attended,
        grad_queries,
        grad_keys,
        grad_values,
        q_total / pair_count,
        k_total / pair_count,
    )


def solution(mesh):
    return jax.shard_map(
        per_device,
        mesh=mesh,
        in_specs=(
            P("fsdp", "seq", "head"),
            P("fsdp", "seq", "head"),
            P("fsdp", "seq", "head"),
            P(),
            P(),
            P("fsdp", "seq", "head"),
            P("fsdp", "seq", None),
        ),
        out_specs=(
            P("fsdp", "seq", "head"),
            P("fsdp", "seq", "head"),
            P("fsdp", "seq", "head"),
            P("fsdp", "seq", "head"),
            P(),
            P(),
        ),
        check_vma=False,
    )
```

```python
import math

import jax
import jax.numpy as jnp
from jax import lax
from jax.sharding import PartitionSpec as P

EPSILON = 1e-06


def extended_2(cells, sides, width):
    for axis, dim in sides:
        count = lax.axis_size(axis)
        ends = count - 1
        head = lax.slice_in_dim(cells, 0, width, axis=dim)
        tail = lax.slice_in_dim(cells, cells.shape[dim] - width, cells.shape[dim], axis=dim)
        cells = jnp.concatenate(
            [
                lax.ppermute(tail, axis, [(i, (i + 1) % count) for i in range(ends)]),
                cells,
                lax.ppermute(head, axis, [((i + 1) % count, i) for i in range(ends)]),
            ],
            axis=dim,
        )
    return cells


def butterfly_sum(value, stages):
    for axes, mask in stages:
        count = math.prod(lax.axis_size(axis) for axis in axes)
        value = value + lax.ppermute(value, axes, [(i, i ^ mask) for i in range(count)])
    return value


def gain_stages():
    seq_count = lax.axis_size("seq")
    head_count = lax.axis_size("head")
    fsdp_count = lax.axis_size("fsdp")
    stages = []
    step = 1
    while step < seq_count:
        stages.append((("seq",), step))
        step *= 2
    stages.append((("head",), 1))
    half = seq_count // 2
    step = 2
    while step < head_count:
        stages.append((("seq", "head"), half * head_count + step))
        step *= 2
    side = math.isqrt(fsdp_count)
    for base in (1, side):
        stages.append((("fsdp",), base))
        stages.append((("fsdp",), 3 * base))
    return stages


def normalize(raw_rows, gain_vector):
    shaped = raw_rows.astype(jnp.float32).reshape(
        raw_rows.shape[0], raw_rows.shape[1], -1, gain_vector.shape[0]
    )
    factor = lax.rsqrt(jnp.mean(shaped * shaped, axis=-1, keepdims=True) + EPSILON)
    unit_rows = shaped * factor
    return (unit_rows, factor, (unit_rows * gain_vector).astype(jnp.bfloat16))


def restore(grad_norm, unit_rows, factor, gain_vector):
    scaled = grad_norm * gain_vector
    inner_mean = jnp.mean(scaled * unit_rows, axis=-1, keepdims=True)
    return factor * (scaled - unit_rows * inner_mean)


def head_pass(operands, allowed, score_scale):
    query_rows, key_rows, value_rows, grad_rows = operands
    scores = (
        jnp.einsum("sqd,skd->sqk", query_rows, key_rows, preferred_element_type=jnp.float32)
        * score_scale
    )
    scores = jnp.where(allowed[:, None, :], scores, -jnp.inf)
    row_max = jnp.max(scores, axis=-1, keepdims=True)
    row_sum = jnp.sum(jnp.exp(scores - row_max), axis=-1, keepdims=True)
    log_total = row_max + jnp.log(row_sum)
    attn_weights = jnp.exp(scores - log_total).astype(jnp.bfloat16)
    attended = jnp.einsum(
        "sqk,skd->sqd", attn_weights, value_rows, preferred_element_type=jnp.float32
    ).astype(jnp.bfloat16)
    row_inner = jnp.sum(
        grad_rows.astype(jnp.float32) * attended.astype(jnp.float32), axis=-1, keepdims=True
    )
    grad_weights = jnp.einsum(
        "sqd,skd->sqk", grad_rows, value_rows, preferred_element_type=jnp.float32
    )
    grad_scores = (attn_weights.astype(jnp.float32) * (grad_weights - row_inner)).astype(
        jnp.bfloat16
    )
    grad_query = (
        jnp.einsum("sqk,skd->sqd", grad_scores, key_rows, preferred_element_type=jnp.float32)
        * score_scale
    )
    return (attended, log_total[..., 0], row_inner[..., 0], grad_query, attn_weights, grad_scores)


def key_terms(grad_scores, attn_weights, query_norm, grad_out, score_scale):
    key_part = (
        jnp.einsum("hsqk,sqhd->skhd", grad_scores, query_norm, preferred_element_type=jnp.float32)
        * score_scale
    )
    value_part = jnp.einsum(
        "hsqk,sqhd->skhd", attn_weights, grad_out, preferred_element_type=jnp.float32
    )
    return (key_part, value_part)


def pack_terms(key_part, value_part):
    sample_count, tile_rows = (key_part.shape[0], key_part.shape[1])
    joined = jnp.concatenate(
        [
            key_part.reshape(sample_count, tile_rows, -1),
            value_part.reshape(sample_count, tile_rows, -1),
        ],
        axis=2,
    )
    return joined.astype(jnp.bfloat16)


def per_device(queries, keys, values, q_gain, k_gain, d_out, window):
    sample_count, tile_rows, columns = queries.shape
    head_size = q_gain.shape[0]
    head_count = columns // head_size
    score_scale = 1.0 / math.sqrt(head_size)
    q_unit, q_factor, q_norm = normalize(queries, q_gain)
    k_unit, k_factor, k_norm = normalize(keys, k_gain)
    packed = jnp.concatenate([keys, values], axis=2)
    tile_count = lax.axis_size("seq")
    ends = tile_count - 1
    from_left = lax.ppermute(packed, "seq", [(i, i + 1) for i in range(ends)])
    from_right = lax.ppermute(packed, "seq", [(i + 1, i) for i in range(ends)])
    left_unit, _, left_norm = normalize(from_left[..., :columns], k_gain)
    right_unit, _, right_norm = normalize(from_right[..., :columns], k_gain)
    k_unit_all = jnp.concatenate([left_unit, k_unit, right_unit], axis=1)
    key_all = jnp.concatenate([left_norm, k_norm, right_norm], axis=1)
    extended = jnp.concatenate([from_left, packed, from_right], axis=1)
    value_all = extended[..., columns:].reshape(sample_count, 3 * tile_rows, head_count, head_size)
    tile_index = lax.axis_index("seq")
    listing = window[:, 0, :]

    def listed(target):
        return jnp.any(listing == target, axis=-1) & (target >= 0) & (target < tile_count)

    left_ok = listed(tile_index - 1)
    right_ok = listed(tile_index + 1)
    block_flags = jnp.stack([left_ok, listed(tile_index), right_ok], axis=1)
    allowed = jnp.repeat(block_flags, tile_rows, axis=1)
    grad_out = d_out.reshape(sample_count, tile_rows, head_count, head_size)
    operands = (
        jnp.moveaxis(q_norm, 2, 0),
        jnp.moveaxis(key_all, 2, 0),
        jnp.moveaxis(value_all, 2, 0),
        jnp.moveaxis(grad_out, 2, 0),
    )
    results = jax.vmap(lambda per_head: head_pass(per_head, allowed, score_scale))(operands)
    attended, log_total, row_inner, grad_query, attn_weights, grad_scores = results
    attended = jnp.moveaxis(attended, 0, 2).reshape(sample_count, tile_rows, columns)
    grad_qnorm = jnp.moveaxis(grad_query, 0, 2)
    key_every, value_every = key_terms(grad_scores, attn_weights, q_norm, grad_out, score_scale)
    left_terms = (key_every[:, :tile_rows], value_every[:, :tile_rows])
    own_terms = (key_every[:, tile_rows : 2 * tile_rows], value_every[:, tile_rows : 2 * tile_rows])
    right_terms = (key_every[:, 2 * tile_rows :], value_every[:, 2 * tile_rows :])
    grad_queries = (
        restore(grad_qnorm, q_unit, q_factor, q_gain)
        .astype(jnp.bfloat16)
        .reshape(sample_count, tile_rows, columns)
    )
    near_terms = jnp.concatenate(
        [
            left_terms[0].astype(jnp.bfloat16).astype(jnp.float32),
            own_terms[0],
            right_terms[0].astype(jnp.bfloat16).astype(jnp.float32),
        ],
        axis=1,
    )
    gain_terms = jnp.concatenate(
        [
            jnp.sum(grad_qnorm * q_unit, axis=(0, 1, 2)),
            jnp.sum(near_terms * k_unit_all, axis=(0, 1, 2)),
        ]
    )
    gain_totals = butterfly_sum(gain_terms, gain_stages())
    from_left = lax.ppermute(
        pack_terms(right_terms[0], right_terms[1]), "seq", [(i, i + 1) for i in range(ends)]
    )
    from_right = lax.ppermute(
        pack_terms(left_terms[0], left_terms[1]), "seq", [(i + 1, i) for i in range(ends)]
    )
    from_left, from_right, gain_totals = lax.optimization_barrier(
        (from_left, from_right, gain_totals)
    )
    incoming = from_left.astype(jnp.float32) + from_right.astype(jnp.float32)
    grad_knorm = own_terms[0] + incoming[..., :columns].reshape(
        sample_count, tile_rows, head_count, head_size
    )
    grad_vsum = own_terms[1] + incoming[..., columns:].reshape(
        sample_count, tile_rows, head_count, head_size
    )
    grad_keys = (
        restore(grad_knorm, k_unit, k_factor, k_gain)
        .astype(jnp.bfloat16)
        .reshape(sample_count, tile_rows, columns)
    )
    grad_values = grad_vsum.astype(jnp.bfloat16).reshape(sample_count, tile_rows, columns)
    q_total, k_total = gain_totals[:head_size], gain_totals[head_size:]
    pair_count = sample_count * lax.axis_size("fsdp") * head_count * lax.axis_size("head")
    return (
        attended,
        grad_queries,
        grad_keys,
        grad_values,
        q_total / pair_count,
        k_total / pair_count,
    )


def solution(mesh):
    return jax.shard_map(
        per_device,
        mesh=mesh,
        in_specs=(
            P("fsdp", "seq", "head"),
            P("fsdp", "seq", "head"),
            P("fsdp", "seq", "head"),
            P(),
            P(),
            P("fsdp", "seq", "head"),
            P("fsdp", "seq", None),
        ),
        out_specs=(
            P("fsdp", "seq", "head"),
            P("fsdp", "seq", "head"),
            P("fsdp", "seq", "head"),
            P("fsdp", "seq", "head"),
            P(),
            P(),
        ),
        check_vma=False,
    )
```

```python
import math

import jax
import jax.numpy as jnp
from jax import lax
from jax.sharding import PartitionSpec as P

EPSILON = 1e-06


def extended_2(cells, sides, width):
    for axis, dim in sides:
        count = lax.axis_size(axis)
        ends = count - 1
        head = lax.slice_in_dim(cells, 0, width, axis=dim)
        tail = lax.slice_in_dim(cells, cells.shape[dim] - width, cells.shape[dim], axis=dim)
        cells = jnp.concatenate(
            [
                lax.ppermute(tail, axis, [(i, (i + 1) % count) for i in range(ends)]),
                cells,
                lax.ppermute(head, axis, [((i + 1) % count, i) for i in range(ends)]),
            ],
            axis=dim,
        )
    return cells


def butterfly_sum(value, stages):
    for axes, mask in stages:
        count = math.prod(lax.axis_size(axis) for axis in axes)
        value = value + lax.ppermute(value, axes, [(i, i ^ mask) for i in range(count)])
    return value


def gain_stages():
    seq_count = lax.axis_size("seq")
    head_count = lax.axis_size("head")
    fsdp_count = lax.axis_size("fsdp")
    stages = []
    step = 1
    while step < seq_count:
        stages.append((("seq",), step))
        step *= 2
    stages.append((("head",), 1))
    half = seq_count // 2
    step = 2
    while step < head_count:
        stages.append((("seq", "head"), half * head_count + step))
        step *= 2
    side = math.isqrt(fsdp_count)
    for base in (1, side):
        stages.append((("fsdp",), base))
        stages.append((("fsdp",), 3 * base))
    return stages


def normalize(raw_rows, gain_vector):
    shaped = raw_rows.astype(jnp.float32).reshape(
        raw_rows.shape[0], raw_rows.shape[1], -1, gain_vector.shape[0]
    )
    factor = lax.rsqrt(jnp.mean(shaped * shaped, axis=-1, keepdims=True) + EPSILON)
    unit_rows = shaped * factor
    return (unit_rows, factor, (unit_rows * gain_vector).astype(jnp.bfloat16))


def restore(grad_norm, unit_rows, factor, gain_vector):
    scaled = grad_norm * gain_vector
    inner_mean = jnp.mean(scaled * unit_rows, axis=-1, keepdims=True)
    return factor * (scaled - unit_rows * inner_mean)


def head_pass(operands, allowed, score_scale):
    query_rows, key_rows, value_rows, grad_rows = operands
    scores = (
        jnp.einsum("sqd,skd->sqk", query_rows, key_rows, preferred_element_type=jnp.float32)
        * score_scale
    )
    scores = jnp.where(allowed[:, None, :], scores, -jnp.inf)
    row_max = jnp.max(scores, axis=-1, keepdims=True)
    row_sum = jnp.sum(jnp.exp(scores - row_max), axis=-1, keepdims=True)
    log_total = row_max + jnp.log(row_sum)
    attn_weights = jnp.exp(scores - log_total).astype(jnp.bfloat16)
    attended = jnp.einsum(
        "sqk,skd->sqd", attn_weights, value_rows, preferred_element_type=jnp.float32
    ).astype(jnp.bfloat16)
    row_inner = jnp.sum(
        grad_rows.astype(jnp.float32) * attended.astype(jnp.float32), axis=-1, keepdims=True
    )
    grad_weights = jnp.einsum(
        "sqd,skd->sqk", grad_rows, value_rows, preferred_element_type=jnp.float32
    )
    grad_scores = (attn_weights.astype(jnp.float32) * (grad_weights - row_inner)).astype(
        jnp.bfloat16
    )
    grad_query = (
        jnp.einsum("sqk,skd->sqd", grad_scores, key_rows, preferred_element_type=jnp.float32)
        * score_scale
    )
    return (attended, log_total[..., 0], row_inner[..., 0], grad_query, attn_weights, grad_scores)


def key_terms(grad_scores, attn_weights, query_norm, grad_out, score_scale):
    key_part = (
        jnp.einsum("hsqk,sqhd->skhd", grad_scores, query_norm, preferred_element_type=jnp.float32)
        * score_scale
    )
    value_part = jnp.einsum(
        "hsqk,sqhd->skhd", attn_weights, grad_out, preferred_element_type=jnp.float32
    )
    return (key_part, value_part)


def pack_terms(key_part, value_part):
    sample_count, tile_rows = (key_part.shape[0], key_part.shape[1])
    joined = jnp.concatenate(
        [
            key_part.reshape(sample_count, tile_rows, -1),
            value_part.reshape(sample_count, tile_rows, -1),
        ],
        axis=2,
    )
    return joined.astype(jnp.bfloat16)


def per_device(queries, keys, values, q_gain, k_gain, d_out, window):
    sample_count, tile_rows, columns = queries.shape
    head_size = q_gain.shape[0]
    head_count = columns // head_size
    score_scale = 1.0 / math.sqrt(head_size)
    q_unit, q_factor, q_norm = normalize(queries, q_gain)
    packed = jnp.concatenate([keys, values], axis=2)
    extended = extended_2(packed, (("seq", 1),), tile_rows)
    k_unit_all, k_factor_all, key_all = normalize(extended[..., :columns], k_gain)
    k_unit = k_unit_all[:, tile_rows : 2 * tile_rows]
    k_factor = k_factor_all[:, tile_rows : 2 * tile_rows]
    value_all = extended[..., columns:].reshape(sample_count, 3 * tile_rows, head_count, head_size)
    tile_index = lax.axis_index("seq")
    tile_count = lax.axis_size("seq")
    listing = window[:, 0, :]

    def listed(target):
        return jnp.any(listing == target, axis=-1) & (target >= 0) & (target < tile_count)

    left_ok = listed(tile_index - 1)
    right_ok = listed(tile_index + 1)
    block_flags = jnp.stack([left_ok, listed(tile_index), right_ok], axis=1)
    allowed = jnp.repeat(block_flags, tile_rows, axis=1)
    grad_out = d_out.reshape(sample_count, tile_rows, head_count, head_size)
    per_head = []
    for head in range(head_count):
        operands = (
            q_norm[:, :, head],
            key_all[:, :, head],
            value_all[:, :, head],
            grad_out[:, :, head],
        )
        attended_h, _, _, grad_query_h, weights_h, grad_scores_h = head_pass(
            operands, allowed, score_scale
        )
        key_h = (
            jnp.einsum(
                "sqk,sqd->skd", grad_scores_h, operands[0], preferred_element_type=jnp.float32
            )
            * score_scale
        )
        value_h = jnp.einsum(
            "sqk,sqd->skd", weights_h, operands[3], preferred_element_type=jnp.float32
        )
        per_head.append((attended_h, grad_query_h, key_h, value_h))
    attended = jnp.concatenate([part[0] for part in per_head], axis=2)
    grad_qnorm = jnp.stack([part[1] for part in per_head], axis=2)
    key_every = jnp.stack([part[2] for part in per_head], axis=2)
    value_every = jnp.stack([part[3] for part in per_head], axis=2)
    left_terms = (key_every[:, :tile_rows], value_every[:, :tile_rows])
    own_terms = (key_every[:, tile_rows : 2 * tile_rows], value_every[:, tile_rows : 2 * tile_rows])
    right_terms = (key_every[:, 2 * tile_rows :], value_every[:, 2 * tile_rows :])
    grad_queries = (
        restore(grad_qnorm, q_unit, q_factor, q_gain)
        .astype(jnp.bfloat16)
        .reshape(sample_count, tile_rows, columns)
    )
    near_terms = jnp.concatenate(
        [
            left_terms[0].astype(jnp.bfloat16).astype(jnp.float32),
            own_terms[0],
            right_terms[0].astype(jnp.bfloat16).astype(jnp.float32),
        ],
        axis=1,
    )
    gain_terms = jnp.concatenate(
        [
            jnp.sum(grad_qnorm * q_unit, axis=(0, 1, 2)),
            jnp.sum(near_terms * k_unit_all, axis=(0, 1, 2)),
        ]
    )
    gain_totals = butterfly_sum(gain_terms, gain_stages())
    ends = tile_count - 1
    from_left = lax.ppermute(
        pack_terms(right_terms[0], right_terms[1]), "seq", [(i, i + 1) for i in range(ends)]
    )
    from_right = lax.ppermute(
        pack_terms(left_terms[0], left_terms[1]), "seq", [(i + 1, i) for i in range(ends)]
    )
    from_left, from_right, gain_totals = lax.optimization_barrier(
        (from_left, from_right, gain_totals)
    )
    incoming = from_left.astype(jnp.float32) + from_right.astype(jnp.float32)
    grad_knorm = own_terms[0] + incoming[..., :columns].reshape(
        sample_count, tile_rows, head_count, head_size
    )
    grad_vsum = own_terms[1] + incoming[..., columns:].reshape(
        sample_count, tile_rows, head_count, head_size
    )
    grad_keys = (
        restore(grad_knorm, k_unit, k_factor, k_gain)
        .astype(jnp.bfloat16)
        .reshape(sample_count, tile_rows, columns)
    )
    grad_values = grad_vsum.astype(jnp.bfloat16).reshape(sample_count, tile_rows, columns)
    q_total, k_total = gain_totals[:head_size], gain_totals[head_size:]
    pair_count = sample_count * lax.axis_size("fsdp") * head_count * lax.axis_size("head")
    return (
        attended,
        grad_queries,
        grad_keys,
        grad_values,
        q_total / pair_count,
        k_total / pair_count,
    )


def solution(mesh):
    return jax.shard_map(
        per_device,
        mesh=mesh,
        in_specs=(
            P("fsdp", "seq", "head"),
            P("fsdp", "seq", "head"),
            P("fsdp", "seq", "head"),
            P(),
            P(),
            P("fsdp", "seq", "head"),
            P("fsdp", "seq", None),
        ),
        out_specs=(
            P("fsdp", "seq", "head"),
            P("fsdp", "seq", "head"),
            P("fsdp", "seq", "head"),
            P("fsdp", "seq", "head"),
            P(),
            P(),
        ),
        check_vma=False,
    )
```

```python
import math

import jax
import jax.numpy as jnp
from jax import lax
from jax.sharding import PartitionSpec as P

EPSILON = 1e-06


def extended_2(cells, sides, width):
    for axis, dim in sides:
        count = lax.axis_size(axis)
        ends = count - 1
        head = lax.slice_in_dim(cells, 0, width, axis=dim)
        tail = lax.slice_in_dim(cells, cells.shape[dim] - width, cells.shape[dim], axis=dim)
        cells = jnp.concatenate(
            [
                lax.ppermute(tail, axis, [(i, (i + 1) % count) for i in range(ends)]),
                cells,
                lax.ppermute(head, axis, [((i + 1) % count, i) for i in range(ends)]),
            ],
            axis=dim,
        )
    return cells


def butterfly_sum(value, stages):
    for axes, mask in stages:
        count = math.prod(lax.axis_size(axis) for axis in axes)
        value = value + lax.ppermute(value, axes, [(i, i ^ mask) for i in range(count)])
    return value


def gain_stages():
    seq_count = lax.axis_size("seq")
    head_count = lax.axis_size("head")
    fsdp_count = lax.axis_size("fsdp")
    stages = []
    step = 1
    while step < seq_count:
        stages.append((("seq",), step))
        step *= 2
    stages.append((("head",), 1))
    half = seq_count // 2
    step = 2
    while step < head_count:
        stages.append((("seq", "head"), half * head_count + step))
        step *= 2
    side = math.isqrt(fsdp_count)
    for base in (1, side):
        stages.append((("fsdp",), base))
        stages.append((("fsdp",), 3 * base))
    return stages


def normalize(raw_rows, gain_vector):
    shaped = raw_rows.astype(jnp.float32).reshape(
        raw_rows.shape[0], raw_rows.shape[1], -1, gain_vector.shape[0]
    )
    factor = lax.rsqrt(jnp.mean(shaped * shaped, axis=-1, keepdims=True) + EPSILON)
    unit_rows = shaped * factor
    return (unit_rows, factor, (unit_rows * gain_vector).astype(jnp.bfloat16))


def restore(grad_norm, unit_rows, factor, gain_vector):
    scaled = grad_norm * gain_vector
    inner_mean = jnp.mean(scaled * unit_rows, axis=-1, keepdims=True)
    return factor * (scaled - unit_rows * inner_mean)


def head_pass(operands, allowed, score_scale):
    query_rows, key_rows, value_rows, grad_rows = operands
    scores = (
        jnp.einsum("sqd,skd->sqk", query_rows, key_rows, preferred_element_type=jnp.float32)
        * score_scale
    )
    scores = jnp.where(allowed[:, None, :], scores, -jnp.inf)
    row_max = jnp.max(scores, axis=-1, keepdims=True)
    row_sum = jnp.sum(jnp.exp(scores - row_max), axis=-1, keepdims=True)
    log_total = row_max + jnp.log(row_sum)
    attn_weights = jnp.exp(scores - log_total).astype(jnp.bfloat16)
    attended = jnp.einsum(
        "sqk,skd->sqd", attn_weights, value_rows, preferred_element_type=jnp.float32
    ).astype(jnp.bfloat16)
    row_inner = jnp.sum(
        grad_rows.astype(jnp.float32) * attended.astype(jnp.float32), axis=-1, keepdims=True
    )
    grad_weights = jnp.einsum(
        "sqd,skd->sqk", grad_rows, value_rows, preferred_element_type=jnp.float32
    )
    grad_scores = (attn_weights.astype(jnp.float32) * (grad_weights - row_inner)).astype(
        jnp.bfloat16
    )
    grad_query = (
        jnp.einsum("sqk,skd->sqd", grad_scores, key_rows, preferred_element_type=jnp.float32)
        * score_scale
    )
    return (attended, log_total[..., 0], row_inner[..., 0], grad_query, attn_weights, grad_scores)


def key_terms(grad_scores, attn_weights, query_norm, grad_out, score_scale):
    key_part = (
        jnp.einsum("hsqk,sqhd->skhd", grad_scores, query_norm, preferred_element_type=jnp.float32)
        * score_scale
    )
    value_part = jnp.einsum(
        "hsqk,sqhd->skhd", attn_weights, grad_out, preferred_element_type=jnp.float32
    )
    return (key_part, value_part)


def pack_terms(key_part, value_part):
    sample_count, tile_rows = (key_part.shape[0], key_part.shape[1])
    joined = jnp.concatenate(
        [
            key_part.reshape(sample_count, tile_rows, -1),
            value_part.reshape(sample_count, tile_rows, -1),
        ],
        axis=2,
    )
    return joined.astype(jnp.bfloat16)


def per_device(queries, keys, values, q_gain, k_gain, d_out, window):
    sample_count, tile_rows, columns = queries.shape
    head_size = q_gain.shape[0]
    head_count = columns // head_size
    score_scale = 1.0 / math.sqrt(head_size)
    q_unit, q_factor, q_norm = normalize(queries, q_gain)
    packed = jnp.concatenate([keys, values], axis=2)
    extended = extended_2(packed, (("seq", 1),), tile_rows)
    k_unit_all, k_factor_all, key_all = normalize(extended[..., :columns], k_gain)
    k_unit = k_unit_all[:, tile_rows : 2 * tile_rows]
    k_factor = k_factor_all[:, tile_rows : 2 * tile_rows]
    value_all = extended[..., columns:].reshape(sample_count, 3 * tile_rows, head_count, head_size)
    tile_index = lax.axis_index("seq")
    tile_count = lax.axis_size("seq")
    listing = window[:, 0, :]

    def listed(target):
        return jnp.any(listing == target, axis=-1) & (target >= 0) & (target < tile_count)

    left_ok = listed(tile_index - 1)
    right_ok = listed(tile_index + 1)
    block_flags = jnp.stack([left_ok, listed(tile_index), right_ok], axis=1)
    allowed = jnp.repeat(block_flags, tile_rows, axis=1)
    grad_out = d_out.reshape(sample_count, tile_rows, head_count, head_size)
    per_head = []
    for head in range(head_count):
        operands = (
            q_norm[:, :, head],
            key_all[:, :, head],
            value_all[:, :, head],
            grad_out[:, :, head],
        )
        attended_h, _, _, grad_query_h, weights_h, grad_scores_h = head_pass(
            operands, allowed, score_scale
        )
        key_h = (
            jnp.einsum(
                "sqk,sqd->skd", grad_scores_h, operands[0], preferred_element_type=jnp.float32
            )
            * score_scale
        )
        value_h = jnp.einsum(
            "sqk,sqd->skd", weights_h, operands[3], preferred_element_type=jnp.float32
        )
        per_head.append((attended_h, grad_query_h, key_h, value_h))
    attended = jnp.concatenate([part[0] for part in per_head], axis=2)
    grad_qnorm = jnp.stack([part[1] for part in per_head], axis=2)
    key_every = jnp.stack([part[2] for part in per_head], axis=2)
    value_every = jnp.stack([part[3] for part in per_head], axis=2)
    left_terms = (key_every[:, :tile_rows], value_every[:, :tile_rows])
    own_terms = (key_every[:, tile_rows : 2 * tile_rows], value_every[:, tile_rows : 2 * tile_rows])
    right_terms = (key_every[:, 2 * tile_rows :], value_every[:, 2 * tile_rows :])
    grad_queries = (
        restore(grad_qnorm, q_unit, q_factor, q_gain)
        .astype(jnp.bfloat16)
        .reshape(sample_count, tile_rows, columns)
    )
    near_terms = jnp.concatenate(
        [
            left_terms[0].astype(jnp.bfloat16).astype(jnp.float32),
            own_terms[0],
            right_terms[0].astype(jnp.bfloat16).astype(jnp.float32),
        ],
        axis=1,
    )
    gain_terms = jnp.concatenate(
        [
            jnp.sum(grad_qnorm * q_unit, axis=(0, 1, 2)),
            jnp.sum(near_terms * k_unit_all, axis=(0, 1, 2)),
        ]
    )
    even = tile_index % 2 == 0
    left_pack = pack_terms(left_terms[0], left_terms[1])
    right_pack = pack_terms(right_terms[0], right_terms[1])
    gain_hi = lax.optimization_barrier(gain_terms.astype(jnp.bfloat16))
    gain_rest = gain_terms - gain_hi.astype(jnp.float32)
    gain_mid = lax.optimization_barrier(gain_rest.astype(jnp.bfloat16))
    gain_lo = lax.optimization_barrier(
        (gain_rest - gain_mid.astype(jnp.float32)).astype(jnp.bfloat16)
    )
    gain_row = jnp.concatenate([gain_hi, gain_mid, gain_lo])
    own_gain = gain_row.astype(jnp.float32).reshape(3, -1)
    width = left_pack.shape[2]
    gain_row = jnp.pad(gain_row, (0, width - gain_row.shape[0])).reshape(1, 1, width)
    gain_row = jnp.broadcast_to(gain_row, (sample_count, 1, width))
    pair_payload = jnp.concatenate([jnp.where(even, right_pack, left_pack), gain_row], axis=1)
    other_payload = jnp.where(even, left_pack, right_pack)
    got_pair = lax.ppermute(pair_payload, "seq", [(i, i ^ 1) for i in range(tile_count)])
    other_pairs = [(i, i + 1 if i % 2 else i - 1) for i in range(tile_count)]
    got_other = lax.ppermute(
        other_payload, "seq", [(i, j) for i, j in other_pairs if 0 <= j < tile_count]
    )
    got_gain = got_pair[0, tile_rows, : 3 * gain_terms.shape[0]].astype(jnp.float32)
    got_gain = got_gain.reshape(3, -1)
    gain_terms = ((own_gain[0] + own_gain[1]) + own_gain[2]) + (
        (got_gain[0] + got_gain[1]) + got_gain[2]
    )
    gain_totals = butterfly_sum(gain_terms, gain_stages()[1:])
    got_pair = got_pair[:, :tile_rows]
    from_left = jnp.where(even, got_other, got_pair)
    from_right = jnp.where(even, got_pair, got_other)
    from_left, from_right, gain_totals = lax.optimization_barrier(
        (from_left, from_right, gain_totals)
    )
    incoming = from_left.astype(jnp.float32) + from_right.astype(jnp.float32)
    grad_knorm = own_terms[0] + incoming[..., :columns].reshape(
        sample_count, tile_rows, head_count, head_size
    )
    grad_vsum = own_terms[1] + incoming[..., columns:].reshape(
        sample_count, tile_rows, head_count, head_size
    )
    grad_keys = (
        restore(grad_knorm, k_unit, k_factor, k_gain)
        .astype(jnp.bfloat16)
        .reshape(sample_count, tile_rows, columns)
    )
    grad_values = grad_vsum.astype(jnp.bfloat16).reshape(sample_count, tile_rows, columns)
    q_total, k_total = gain_totals[:head_size], gain_totals[head_size:]
    pair_count = sample_count * lax.axis_size("fsdp") * head_count * lax.axis_size("head")
    return (
        attended,
        grad_queries,
        grad_keys,
        grad_values,
        q_total / pair_count,
        k_total / pair_count,
    )


def solution(mesh):
    return jax.shard_map(
        per_device,
        mesh=mesh,
        in_specs=(
            P("fsdp", "seq", "head"),
            P("fsdp", "seq", "head"),
            P("fsdp", "seq", "head"),
            P(),
            P(),
            P("fsdp", "seq", "head"),
            P("fsdp", "seq", None),
        ),
        out_specs=(
            P("fsdp", "seq", "head"),
            P("fsdp", "seq", "head"),
            P("fsdp", "seq", "head"),
            P("fsdp", "seq", "head"),
            P(),
            P(),
        ),
        check_vma=False,
    )
```

```python
import math

import jax
import jax.numpy as jnp
from jax import lax
from jax.sharding import PartitionSpec as P

EPSILON = 1e-06


def extended_2(cells, sides, width):
    for axis, dim in sides:
        count = lax.axis_size(axis)
        ends = count - 1
        head = lax.slice_in_dim(cells, 0, width, axis=dim)
        tail = lax.slice_in_dim(cells, cells.shape[dim] - width, cells.shape[dim], axis=dim)
        cells = jnp.concatenate(
            [
                lax.ppermute(tail, axis, [(i, (i + 1) % count) for i in range(ends)]),
                cells,
                lax.ppermute(head, axis, [((i + 1) % count, i) for i in range(ends)]),
            ],
            axis=dim,
        )
    return cells


def butterfly_sum(value, stages):
    for axes, mask in stages:
        count = math.prod(lax.axis_size(axis) for axis in axes)
        value = value + lax.ppermute(value, axes, [(i, i ^ mask) for i in range(count)])
    return value


def gain_stages():
    seq_count = lax.axis_size("seq")
    head_count = lax.axis_size("head")
    fsdp_count = lax.axis_size("fsdp")
    stages = []
    step = 1
    while step < seq_count:
        stages.append((("seq",), step))
        step *= 2
    stages.append((("head",), 1))
    half = seq_count // 2
    step = 2
    while step < head_count:
        stages.append((("seq", "head"), half * head_count + step))
        step *= 2
    side = math.isqrt(fsdp_count)
    for base in (1, side):
        stages.append((("fsdp",), base))
        stages.append((("fsdp",), 3 * base))
    return stages


def normalize(raw_rows, gain_vector):
    shaped = raw_rows.astype(jnp.float32).reshape(
        raw_rows.shape[0], raw_rows.shape[1], -1, gain_vector.shape[0]
    )
    factor = lax.rsqrt(jnp.mean(shaped * shaped, axis=-1, keepdims=True) + EPSILON)
    unit_rows = shaped * factor
    return (unit_rows, factor, (unit_rows * gain_vector).astype(jnp.bfloat16))


def restore(grad_norm, unit_rows, factor, gain_vector):
    scaled = grad_norm * gain_vector
    inner_mean = jnp.mean(scaled * unit_rows, axis=-1, keepdims=True)
    return factor * (scaled - unit_rows * inner_mean)


def head_pass(operands, allowed, score_scale):
    query_rows, key_rows, value_rows, grad_rows = operands
    scores = (
        jnp.einsum("sqd,skd->sqk", query_rows, key_rows, preferred_element_type=jnp.float32)
        * score_scale
    )
    scores = jnp.where(allowed[:, None, :], scores, -jnp.inf)
    row_max = jnp.max(scores, axis=-1, keepdims=True)
    row_sum = jnp.sum(jnp.exp(scores - row_max), axis=-1, keepdims=True)
    log_total = row_max + jnp.log(row_sum)
    attn_weights = jnp.exp(scores - log_total).astype(jnp.bfloat16)
    attended = jnp.einsum(
        "sqk,skd->sqd", attn_weights, value_rows, preferred_element_type=jnp.float32
    ).astype(jnp.bfloat16)
    row_inner = jnp.sum(
        grad_rows.astype(jnp.float32) * attended.astype(jnp.float32), axis=-1, keepdims=True
    )
    grad_weights = jnp.einsum(
        "sqd,skd->sqk", grad_rows, value_rows, preferred_element_type=jnp.float32
    )
    grad_scores = (attn_weights.astype(jnp.float32) * (grad_weights - row_inner)).astype(
        jnp.bfloat16
    )
    grad_query = (
        jnp.einsum("sqk,skd->sqd", grad_scores, key_rows, preferred_element_type=jnp.float32)
        * score_scale
    )
    return (attended, log_total[..., 0], row_inner[..., 0], grad_query, attn_weights, grad_scores)


def key_terms(grad_scores, attn_weights, query_norm, grad_out, score_scale):
    key_part = (
        jnp.einsum("hsqk,sqhd->skhd", grad_scores, query_norm, preferred_element_type=jnp.float32)
        * score_scale
    )
    value_part = jnp.einsum(
        "hsqk,sqhd->skhd", attn_weights, grad_out, preferred_element_type=jnp.float32
    )
    return (key_part, value_part)


def pack_terms(key_part, value_part):
    sample_count, tile_rows = (key_part.shape[0], key_part.shape[1])
    joined = jnp.concatenate(
        [
            key_part.reshape(sample_count, tile_rows, -1),
            value_part.reshape(sample_count, tile_rows, -1),
        ],
        axis=2,
    )
    return joined.astype(jnp.bfloat16)


def per_device(queries, keys, values, q_gain, k_gain, d_out, window):
    sample_count, tile_rows, columns = queries.shape
    head_size = q_gain.shape[0]
    head_count = columns // head_size
    score_scale = 1.0 / math.sqrt(head_size)
    q_unit, q_factor, q_norm = normalize(queries, q_gain)
    packed = jnp.concatenate([keys, values], axis=2)
    extended = extended_2(packed, (("seq", 1),), tile_rows)
    k_unit_all, k_factor_all, key_all = normalize(extended[..., :columns], k_gain)
    k_unit = k_unit_all[:, tile_rows : 2 * tile_rows]
    k_factor = k_factor_all[:, tile_rows : 2 * tile_rows]
    value_all = extended[..., columns:].reshape(sample_count, 3 * tile_rows, head_count, head_size)
    tile_index = lax.axis_index("seq")
    tile_count = lax.axis_size("seq")
    listing = window[:, 0, :]

    def listed(target):
        return jnp.any(listing == target, axis=-1) & (target >= 0) & (target < tile_count)

    left_ok = listed(tile_index - 1)
    right_ok = listed(tile_index + 1)
    block_flags = jnp.stack([left_ok, listed(tile_index), right_ok], axis=1)
    allowed = jnp.repeat(block_flags, tile_rows, axis=1)
    grad_out = d_out.reshape(sample_count, tile_rows, head_count, head_size)
    per_head = []
    for head in range(head_count):
        operands = (
            q_norm[:, :, head],
            key_all[:, :, head],
            value_all[:, :, head],
            grad_out[:, :, head],
        )
        attended_h, _, _, grad_query_h, weights_h, grad_scores_h = head_pass(
            operands, allowed, score_scale
        )
        key_h = (
            jnp.einsum(
                "sqk,sqd->skd", grad_scores_h, operands[0], preferred_element_type=jnp.float32
            )
            * score_scale
        )
        value_h = jnp.einsum(
            "sqk,sqd->skd", weights_h, operands[3], preferred_element_type=jnp.float32
        )
        per_head.append((attended_h, grad_query_h, key_h, value_h))
    attended = jnp.concatenate([part[0] for part in per_head], axis=2)
    grad_qnorm = jnp.stack([part[1] for part in per_head], axis=2)
    key_every = jnp.stack([part[2] for part in per_head], axis=2)
    value_every = jnp.stack([part[3] for part in per_head], axis=2)
    left_terms = (key_every[:, :tile_rows], value_every[:, :tile_rows])
    own_terms = (key_every[:, tile_rows : 2 * tile_rows], value_every[:, tile_rows : 2 * tile_rows])
    right_terms = (key_every[:, 2 * tile_rows :], value_every[:, 2 * tile_rows :])
    grad_queries = (
        restore(grad_qnorm, q_unit, q_factor, q_gain)
        .astype(jnp.bfloat16)
        .reshape(sample_count, tile_rows, columns)
    )
    near_terms = jnp.concatenate(
        [
            left_terms[0].astype(jnp.bfloat16).astype(jnp.float32),
            own_terms[0],
            right_terms[0].astype(jnp.bfloat16).astype(jnp.float32),
        ],
        axis=1,
    )
    gain_terms = jnp.concatenate(
        [
            jnp.sum(grad_qnorm * q_unit, axis=(0, 1, 2)),
            jnp.sum(near_terms * k_unit_all, axis=(0, 1, 2)),
        ]
    )
    stages = gain_stages()
    off_plane = len(stages) - 4
    gain_totals = butterfly_sum(gain_terms, stages[:off_plane])
    ends = tile_count - 1
    from_left = lax.ppermute(
        pack_terms(right_terms[0], right_terms[1]), "seq", [(i, i + 1) for i in range(ends)]
    )
    from_right = lax.ppermute(
        pack_terms(left_terms[0], left_terms[1]), "seq", [(i + 1, i) for i in range(ends)]
    )
    from_left, from_right, gain_totals = lax.optimization_barrier(
        (from_left, from_right, gain_totals)
    )
    gain_totals = butterfly_sum(gain_totals, stages[off_plane:])
    incoming = from_left.astype(jnp.float32) + from_right.astype(jnp.float32)
    grad_knorm = own_terms[0] + incoming[..., :columns].reshape(
        sample_count, tile_rows, head_count, head_size
    )
    grad_vsum = own_terms[1] + incoming[..., columns:].reshape(
        sample_count, tile_rows, head_count, head_size
    )
    grad_keys = (
        restore(grad_knorm, k_unit, k_factor, k_gain)
        .astype(jnp.bfloat16)
        .reshape(sample_count, tile_rows, columns)
    )
    grad_values = grad_vsum.astype(jnp.bfloat16).reshape(sample_count, tile_rows, columns)
    q_total, k_total = gain_totals[:head_size], gain_totals[head_size:]
    pair_count = sample_count * lax.axis_size("fsdp") * head_count * lax.axis_size("head")
    return (
        attended,
        grad_queries,
        grad_keys,
        grad_values,
        q_total / pair_count,
        k_total / pair_count,
    )


def solution(mesh):
    return jax.shard_map(
        per_device,
        mesh=mesh,
        in_specs=(
            P("fsdp", "seq", "head"),
            P("fsdp", "seq", "head"),
            P("fsdp", "seq", "head"),
            P(),
            P(),
            P("fsdp", "seq", "head"),
            P("fsdp", "seq", None),
        ),
        out_specs=(
            P("fsdp", "seq", "head"),
            P("fsdp", "seq", "head"),
            P("fsdp", "seq", "head"),
            P("fsdp", "seq", "head"),
            P(),
            P(),
        ),
        check_vma=False,
    )
```

```python
import math

import jax
import jax.numpy as jnp
from jax import lax
from jax.sharding import PartitionSpec as P

EPSILON = 1e-06


def extended_2(cells, sides, width):
    for axis, dim in sides:
        count = lax.axis_size(axis)
        ends = count - 1
        head = lax.slice_in_dim(cells, 0, width, axis=dim)
        tail = lax.slice_in_dim(cells, cells.shape[dim] - width, cells.shape[dim], axis=dim)
        cells = jnp.concatenate(
            [
                lax.ppermute(tail, axis, [(i, (i + 1) % count) for i in range(ends)]),
                cells,
                lax.ppermute(head, axis, [((i + 1) % count, i) for i in range(ends)]),
            ],
            axis=dim,
        )
    return cells


def butterfly_sum(value, stages):
    for axes, mask in stages:
        count = math.prod(lax.axis_size(axis) for axis in axes)
        value = value + lax.ppermute(value, axes, [(i, i ^ mask) for i in range(count)])
    return value


def gain_stages():
    seq_count = lax.axis_size("seq")
    head_count = lax.axis_size("head")
    fsdp_count = lax.axis_size("fsdp")
    stages = [(("head",), 1)]
    half = seq_count // 2
    step = 2
    while step < head_count:
        stages.append((("seq", "head"), half * head_count + step))
        step *= 2
    step = 1
    while step < seq_count:
        stages.append((("seq",), step))
        step *= 2
    side = math.isqrt(fsdp_count)
    for base in (1, side):
        stages.append((("fsdp",), base))
        stages.append((("fsdp",), 3 * base))
    return stages


def normalize(raw_rows, gain_vector):
    shaped = raw_rows.astype(jnp.float32).reshape(
        raw_rows.shape[0], raw_rows.shape[1], -1, gain_vector.shape[0]
    )
    factor = lax.rsqrt(jnp.mean(shaped * shaped, axis=-1, keepdims=True) + EPSILON)
    unit_rows = shaped * factor
    return (unit_rows, factor, (unit_rows * gain_vector).astype(jnp.bfloat16))


def restore(grad_norm, unit_rows, factor, gain_vector):
    scaled = grad_norm * gain_vector
    inner_mean = jnp.mean(scaled * unit_rows, axis=-1, keepdims=True)
    return factor * (scaled - unit_rows * inner_mean)


def head_pass(operands, allowed, score_scale):
    query_rows, key_rows, value_rows, grad_rows = operands
    scores = (
        jnp.einsum("sqd,skd->sqk", query_rows, key_rows, preferred_element_type=jnp.float32)
        * score_scale
    )
    scores = jnp.where(allowed[:, None, :], scores, -jnp.inf)
    row_max = jnp.max(scores, axis=-1, keepdims=True)
    row_sum = jnp.sum(jnp.exp(scores - row_max), axis=-1, keepdims=True)
    log_total = row_max + jnp.log(row_sum)
    attn_weights = jnp.exp(scores - log_total).astype(jnp.bfloat16)
    attended = jnp.einsum(
        "sqk,skd->sqd", attn_weights, value_rows, preferred_element_type=jnp.float32
    ).astype(jnp.bfloat16)
    row_inner = jnp.sum(
        grad_rows.astype(jnp.float32) * attended.astype(jnp.float32), axis=-1, keepdims=True
    )
    grad_weights = jnp.einsum(
        "sqd,skd->sqk", grad_rows, value_rows, preferred_element_type=jnp.float32
    )
    grad_scores = (attn_weights.astype(jnp.float32) * (grad_weights - row_inner)).astype(
        jnp.bfloat16
    )
    grad_query = (
        jnp.einsum("sqk,skd->sqd", grad_scores, key_rows, preferred_element_type=jnp.float32)
        * score_scale
    )
    return (attended, log_total[..., 0], row_inner[..., 0], grad_query, attn_weights, grad_scores)


def key_terms(grad_scores, attn_weights, query_norm, grad_out, score_scale):
    key_part = (
        jnp.einsum("hsqk,sqhd->skhd", grad_scores, query_norm, preferred_element_type=jnp.float32)
        * score_scale
    )
    value_part = jnp.einsum(
        "hsqk,sqhd->skhd", attn_weights, grad_out, preferred_element_type=jnp.float32
    )
    return (key_part, value_part)


def pack_terms(key_part, value_part):
    sample_count, tile_rows = (key_part.shape[0], key_part.shape[1])
    joined = jnp.concatenate(
        [
            key_part.reshape(sample_count, tile_rows, -1),
            value_part.reshape(sample_count, tile_rows, -1),
        ],
        axis=2,
    )
    return joined.astype(jnp.bfloat16)


def per_device(queries, keys, values, q_gain, k_gain, d_out, window):
    sample_count, tile_rows, columns = queries.shape
    head_size = q_gain.shape[0]
    head_count = columns // head_size
    score_scale = 1.0 / math.sqrt(head_size)
    q_unit, q_factor, q_norm = normalize(queries, q_gain)
    packed = jnp.concatenate([keys, values], axis=2)
    extended = extended_2(packed, (("seq", 1),), tile_rows)
    k_unit_all, k_factor_all, key_all = normalize(extended[..., :columns], k_gain)
    k_unit = k_unit_all[:, tile_rows : 2 * tile_rows]
    k_factor = k_factor_all[:, tile_rows : 2 * tile_rows]
    value_all = extended[..., columns:].reshape(sample_count, 3 * tile_rows, head_count, head_size)
    tile_index = lax.axis_index("seq")
    tile_count = lax.axis_size("seq")
    listing = window[:, 0, :]

    def listed(target):
        return jnp.any(listing == target, axis=-1) & (target >= 0) & (target < tile_count)

    left_ok = listed(tile_index - 1)
    right_ok = listed(tile_index + 1)
    block_flags = jnp.stack([left_ok, listed(tile_index), right_ok], axis=1)
    allowed = jnp.repeat(block_flags, tile_rows, axis=1)
    grad_out = d_out.reshape(sample_count, tile_rows, head_count, head_size)
    per_head = []
    for head in range(head_count):
        operands = (
            q_norm[:, :, head],
            key_all[:, :, head],
            value_all[:, :, head],
            grad_out[:, :, head],
        )
        attended_h, _, _, grad_query_h, weights_h, grad_scores_h = head_pass(
            operands, allowed, score_scale
        )
        key_h = (
            jnp.einsum(
                "sqk,sqd->skd", grad_scores_h, operands[0], preferred_element_type=jnp.float32
            )
            * score_scale
        )
        value_h = jnp.einsum(
            "sqk,sqd->skd", weights_h, operands[3], preferred_element_type=jnp.float32
        )
        per_head.append((attended_h, grad_query_h, key_h, value_h))
    attended = jnp.concatenate([part[0] for part in per_head], axis=2)
    grad_qnorm = jnp.stack([part[1] for part in per_head], axis=2)
    key_every = jnp.stack([part[2] for part in per_head], axis=2)
    value_every = jnp.stack([part[3] for part in per_head], axis=2)
    left_terms = (key_every[:, :tile_rows], value_every[:, :tile_rows])
    own_terms = (key_every[:, tile_rows : 2 * tile_rows], value_every[:, tile_rows : 2 * tile_rows])
    right_terms = (key_every[:, 2 * tile_rows :], value_every[:, 2 * tile_rows :])
    grad_queries = (
        restore(grad_qnorm, q_unit, q_factor, q_gain)
        .astype(jnp.bfloat16)
        .reshape(sample_count, tile_rows, columns)
    )
    near_terms = jnp.concatenate(
        [
            left_terms[0].astype(jnp.bfloat16).astype(jnp.float32),
            own_terms[0],
            right_terms[0].astype(jnp.bfloat16).astype(jnp.float32),
        ],
        axis=1,
    )
    gain_terms = jnp.concatenate(
        [
            jnp.sum(grad_qnorm * q_unit, axis=(0, 1, 2)),
            jnp.sum(near_terms * k_unit_all, axis=(0, 1, 2)),
        ]
    )
    gain_totals = butterfly_sum(gain_terms, gain_stages())
    ends = tile_count - 1
    from_left = lax.ppermute(
        pack_terms(right_terms[0], right_terms[1]), "seq", [(i, i + 1) for i in range(ends)]
    )
    from_right = lax.ppermute(
        pack_terms(left_terms[0], left_terms[1]), "seq", [(i + 1, i) for i in range(ends)]
    )
    from_left, from_right, gain_totals = lax.optimization_barrier(
        (from_left, from_right, gain_totals)
    )
    incoming = from_left.astype(jnp.float32) + from_right.astype(jnp.float32)
    grad_knorm = own_terms[0] + incoming[..., :columns].reshape(
        sample_count, tile_rows, head_count, head_size
    )
    grad_vsum = own_terms[1] + incoming[..., columns:].reshape(
        sample_count, tile_rows, head_count, head_size
    )
    grad_keys = (
        restore(grad_knorm, k_unit, k_factor, k_gain)
        .astype(jnp.bfloat16)
        .reshape(sample_count, tile_rows, columns)
    )
    grad_values = grad_vsum.astype(jnp.bfloat16).reshape(sample_count, tile_rows, columns)
    q_total, k_total = gain_totals[:head_size], gain_totals[head_size:]
    pair_count = sample_count * lax.axis_size("fsdp") * head_count * lax.axis_size("head")
    return (
        attended,
        grad_queries,
        grad_keys,
        grad_values,
        q_total / pair_count,
        k_total / pair_count,
    )


def solution(mesh):
    return jax.shard_map(
        per_device,
        mesh=mesh,
        in_specs=(
            P("fsdp", "seq", "head"),
            P("fsdp", "seq", "head"),
            P("fsdp", "seq", "head"),
            P(),
            P(),
            P("fsdp", "seq", "head"),
            P("fsdp", "seq", None),
        ),
        out_specs=(
            P("fsdp", "seq", "head"),
            P("fsdp", "seq", "head"),
            P("fsdp", "seq", "head"),
            P("fsdp", "seq", "head"),
            P(),
            P(),
        ),
        check_vma=False,
    )
```
